32 devices in a mesh: req: 8 (over z, x), head: 4 (over y, core).
Axes of the slice: x: 2, y: 2, z: 4, core: 2. Of those that a mesh axis runs over, the one named last changes fastest.
Arguments:
- tokens: bfloat16 [256, 2048], P('req'), may hold values from -6 to 6
- norm_gain: float32 [2048], replicated, may hold values from 0.1 to 1.9
- key_value_weight: bfloat16 [2048, 16, 2, 128], P(None, 'head'), may hold values from -0.125 to 0.125
- query_weight: bfloat16 [32, 2048, 512], P('req', None, 'head'), may hold values from -0.125 to 0.125
- output_weight: bfloat16 [32, 512, 2048], P('req', 'head'), may hold values from -0.5 to 0.5
- cache_keys: bfloat16 [512, 128, 16, 128], P('req', None, 'head'), may hold values from -552 to 552
- cache_values: bfloat16 [512, 128, 16, 128], P('req', None, 'head'), may hold values from -6 to 6
- cache_length: int32 [256], P('req'), may hold values from 16 to 4096, as said below
- page_table: int32 [256, 32], P('req'), may hold values from 0 to 511, as said below
- expert_choice: int32 [256, 2], P('req'), may hold values from 0 to 7, all different within a row; in each aligned block of 32 rows (0 to 31, 32 to 63, ...) at most 12 rows name the same one
- expert_gate: float32 [256, 2], P('req'), may hold values from 0.1 to 1
- live_mask: int32 [256], P('req'), may hold values 0 or 1
Outputs:
- attention_out: bfloat16 [256, 2048], P('req', 'head')
The draws below stay inside these ranges and needn't reach their ends.
Inputs may be any that keep to these rules, and one draw needn't show every extreme that they name: `cache_length`: request group g holds requests g * 32 to (g+1) * 32 - 1. Every request holds 16 to 64 cached tokens, except that in 3 * (number of groups) // 4 groups exactly one request holds 2048 to 4096; some request holds exactly 4096. `page_table`: group g owns pages g * 64 to (g+1) * 64 - 1, and row r lists, in order, the ceil(cache_length[r] / 128) distinct pages of request r, all owned by its group; no page serves two requests; later entries repeat the request's first page. A group uses at most 63 pages, and some group uses exactly that many. `expert_choice`: among the tokens of one request group, no attention expert is chosen more than 12 times, and in some group one expert is chosen exactly 12 times; a token's choices differ.
All inputs are finite; a program needn't handle non-finite values. No bound on the sum of `live_mask` on one device may be relied on, other than what follows from the above.
Results may differ from the reference program's by a relative error of at most 0.007.
The reference program's roundings to bfloat16 on the way count: a program that leaves them out, or rounds other values in their place, can miss the bound.
Values may be sent and summed in bfloat16 or wider, within the bound.
No kernel may reach another device: no remote copies, remote signals or barrier semaphores. Data moves between devices by JAX's collectives and lax.ppermute only.
A program may use at most 128 MiB of HBM per device.

```python
import math
import jax
import jax.numpy as jnp
import numpy as np
from jax import lax

D = 2048
HEADS = 16
HD = 128
AEXP = 8
TOPK = 2
PAGE = 128
SHORT_MIN = 16
SHORT_MAX = 64
LONG_MIN = 2048
LONG_MAX = 4096
REQ_DEV = 32
REQS = 256
CAP = 12
MAXP = 32
PAGES_DEV = 64
PAGES = 512
HPD = 4
N_HEAD = 4


def layout_draw(key):
    groups = REQS // REQ_DEV
    base_key = jax.random.fold_in(key, 11)
    key_one, key_two, key_three, key_four, key_five = jax.random.split(base_key, 5)
    short_length = jax.random.randint(key_one, (groups, REQ_DEV), SHORT_MIN, SHORT_MAX + 1)
    long_length = jax.random.randint(key_two, (groups,), LONG_MIN, LONG_MAX + 1)
    order = jax.random.permutation(key_three, groups)
    has_long = order < 3 * groups // 4
    long_length = jnp.where(order == 0, LONG_MAX, long_length)
    where_long = jax.random.randint(key_four, (groups,), 0, REQ_DEV)
    slot_ids = jnp.arange(REQ_DEV)
    is_long = has_long[:, None] & (slot_ids[None, :] == where_long[:, None])
    lengths = jnp.where(is_long, long_length[:, None], short_length)
    pages_needed = (lengths + PAGE - 1) // PAGE
    offset = jnp.cumsum(pages_needed, axis=1) - pages_needed
    shuffled = jax.vmap(lambda sub_key: jax.random.permutation(sub_key, PAGES_DEV))(jax.random.split(key_five, groups))
    first_value = shuffled[:, :1]
    position = jnp.arange(PAGES_DEV)[None, :]
    shuffled = jnp.where(shuffled == PAGES_DEV - 1, first_value, shuffled)
    shuffled = jnp.where(position == 0, PAGES_DEV - 1, shuffled)
    entry = jnp.arange(MAXP)[None, None, :]
    index = offset[:, :, None] + jnp.where(entry < pages_needed[:, :, None], entry, 0)
    local_pages = jax.vmap(lambda table_perm, table_index: table_perm[table_index])(shuffled, index)
    table = local_pages + (jnp.arange(groups) * PAGES_DEV)[:, None, None]
    return (lengths.reshape(REQS).astype(jnp.int32), table.reshape(REQS, MAXP).astype(jnp.int32))


def draw_cache_length(key, part):
    return layout_draw(key)[0]


def draw_page_table(key, part):
    return layout_draw(key)[1]


def draw_cache_keys(key, part):
    shape = (PAGES, PAGE, HEADS, HD)
    base = jnp.clip(jax.random.normal(key, shape, jnp.float32), -6.0, 6.0)
    return base.astype(jnp.bfloat16)


def with_ends(entries, key, smallest, largest):
    place = [jax.random.randint(jax.random.fold_in(key, axis), (), 0, length) for axis, length in enumerate(entries.shape)]
    widest = entries.shape.index(max(entries.shape))
    beside = place[:widest] + [(place[widest] + 1) % entries.shape[widest]] + place[widest + 1:]
    return entries.at[tuple(place)].set(smallest).at[tuple(beside)].set(largest)


def steps_of(rng, dims, pieces, smallest, high):
    def one(axis_at, blocks):
        draws = jax.random.uniform(jax.random.fold_in(jax.random.fold_in(rng, 6), axis_at), (blocks,), jnp.float32, smallest / len(pieces), high / len(pieces))
        return jnp.repeat(jnp.exp(draws), dims[axis_at] // blocks).reshape((-1,) + (1,) * (len(dims) - axis_at - 1))

    gain = one(*pieces[0])
    for cut in pieces[1:]:
        gain = gain * one(*cut)
    return gain


def deal_out(own_key, own, number, rows, amount, top, bound, slope):
    sequence = jax.random.permutation(own_key, amount)
    heavy_load, usual = load_shares(amount, rows * top, bound, slope, True), load_shares(amount, rows * top, bound, slope, False)
    places = jnp.arange(amount)

    def named(sizes, rotation):
        used = int((sizes > 0).sum())
        fixed = max(1, used // 4)
        passed = fixed + (places - fixed + rotation * (used - fixed)) % max(1, amount - fixed)
        return jnp.zeros((amount,), jnp.int32).at[sequence[jnp.where(places < fixed, places, passed)]].set(jnp.asarray(sizes, jnp.int32))

    sizes = jnp.where(number % 4 == 0, named(heavy_load, number // 4), named(usual, number - number // 4 - 1))
    mixed = jax.random.permutation(jax.random.fold_in(own, 3), amount)
    donor, taker = mixed[0:amount // 2 * 2:2], mixed[1:amount // 2 * 2:2]
    margin = jnp.minimum(sizes[donor] - 1, bound - sizes[taker]) // 2
    margin = jnp.where((donor == sequence[0]) | (taker == sequence[0]) | (sizes[taker] == 0), 0, jnp.maximum(margin, 0))
    passed = jax.random.randint(jax.random.fold_in(own, 4), (amount // 2,), 0, 1 << 20) % (margin + 1)
    sizes = sizes.at[donor].add(-passed).at[taker].add(passed)
    members = jnp.searchsorted(jnp.cumsum(sizes), jnp.arange(rows * top), side="right").astype(jnp.int32)
    table = members.reshape(top, rows).T
    table = table[jax.random.permutation(jax.random.fold_in(own, 1), rows)]
    rotation = jax.random.randint(jax.random.fold_in(own, 2), (rows, 1), 0, top)
    return jnp.take_along_axis(table, (jnp.arange(top)[None, :] + rotation) % top, axis=1)


def load_shares(count, total, most, skew, full):
    portions = [(1 << 20) // math.isqrt(grade ** skew) + 1 for grade in range(1, count + 1)]
    largest = most if full else min(most, max(-(-total // count), total * portions[0] // sum(portions)))
    least = 1 if total - largest >= count - 1 else 0
    given, rest = [largest] + [least] * (count - 1), total - largest - least * (count - 1)
    while rest > 0:
        free = [i for i in range(1, count) if given[i] < largest] or [i for i in range(1, count) if given[i] < most]
        pool, budget = sum([portions[i] for i in free]), rest
        for i in free:
            extra = min(most - given[i], max(1, budget * portions[i] // pool), rest)
            given[i] = given[i] + extra
            rest = rest - extra
    return np.array(given)


def scatter_about(stream_key, extent, width, limit, pieces=(), kind=jnp.bfloat16):
    factor_of = steps_of(stream_key, extent, pieces, -0.22, 0.18) if pieces else 1.0
    values = jax.random.normal(stream_key, extent, jnp.float32) * width * factor_of
    return jnp.minimum(jnp.maximum(values, -limit), limit).astype(kind)


def setup_inputs(seed: int = 0) -> dict:
    arg_keys = jax.random.split(jax.random.key(seed), 13)
    tokens = scatter_about(arg_keys[0], (REQS, D), 1.0, 6.0, ((0, 8),))
    norm_gain = jnp.clip(1.0 + 0.18 * jax.random.normal(arg_keys[1], (D,), jnp.float32), 0.1, 1.9)
    key_value_weight = scatter_about(arg_keys[2], (D, HEADS, 2, HD), D ** -0.5, 0.125, ((1, 4),))
    query_weight = scatter_about(arg_keys[3], (AEXP * HPD, D, N_HEAD * HD), D ** -0.5, 0.125, ((0, 8), (2, 4)))
    output_weight = scatter_about(arg_keys[4], (AEXP * HPD, N_HEAD * HD, D), HD ** -0.5, 0.5, ((0, 8), (1, 4)))
    cache_keys = draw_cache_keys(jax.random.fold_in(arg_keys[12], 71), 0)
    cache_values = scatter_about(arg_keys[6], (PAGES, PAGE, HEADS, HD), 1.0, 6.0, ((0, 8), (2, 4)))
    cache_length = draw_cache_length(jax.random.fold_in(arg_keys[12], 71), 0)
    page_table = draw_page_table(jax.random.fold_in(arg_keys[12], 71), 0)
    expert_choice_keys = jax.random.split(jax.random.fold_in(arg_keys[9], 1), REQS // REQ_DEV)
    expert_choice_turns = jax.random.permutation(jax.random.fold_in(arg_keys[9], 3), REQS // REQ_DEV)
    expert_choice = jax.vmap(lambda own, number: deal_out(jax.random.fold_in(arg_keys[9], 2), own, number, REQ_DEV, AEXP, TOPK, CAP, 2))(expert_choice_keys, expert_choice_turns).reshape((REQS, TOPK))
    expert_gate = jnp.clip(0.1 + 0.9 * jax.random.uniform(arg_keys[10], (REQS, TOPK), jnp.float32) ** steps_of(arg_keys[10], (REQS, TOPK), ((0, 8),), -0.2, 0.2), 0.1, 1.0)
    live_mask = with_ends((jax.random.randint(arg_keys[11], (REQS,), 0, 8) < 7).astype(jnp.int32), jax.random.fold_in(arg_keys[11], 1), 0, 1)
    return {"tokens": tokens, "norm_gain": norm_gain, "key_value_weight": key_value_weight, "query_weight": query_weight, "output_weight": output_weight, "cache_keys": cache_keys, "cache_values": cache_values, "cache_length": cache_length, "page_table": page_table, "expert_choice": expert_choice, "expert_gate": expert_gate, "live_mask": live_mask}


eps = 1e-06
theta = 10000.0

def rotate(vectors, positions):
    half_width = vectors.shape[-1] // 2
    frequency = theta ** (-(jnp.arange(half_width, dtype=jnp.float32) * 2.0) / vectors.shape[-1])
    angles = positions.astype(jnp.float32)[..., None] * frequency
    cosine = jnp.cos(angles)
    sine_part = jnp.sin(angles)
    first_half = vectors[..., :half_width]
    second = vectors[..., half_width:]
    return jnp.concatenate([first_half * cosine - second * sine_part, second * cosine + first_half * sine_part], axis=-1)

def reference(tokens, norm_gain, key_value_weight, query_weight, output_weight, cache_keys, cache_values, cache_length, page_table, expert_choice, expert_gate, live_mask):
    hpd_count = HEADS // N_HEAD
    as_float = tokens.astype(jnp.float32)
    normed = (as_float * lax.rsqrt(lax.optimization_barrier(jnp.mean(as_float * as_float, axis=-1, keepdims=True)) + eps) * norm_gain).astype(jnp.bfloat16)
    key_value = jnp.dot(normed, key_value_weight.reshape(D, HEADS * 2 * HD), preferred_element_type=jnp.float32).reshape(REQS, HEADS, 2, HD)
    key_new = rotate(key_value[:, :, 0], cache_length[:, None]).astype(jnp.bfloat16)
    value_new = key_value[:, :, 1].astype(jnp.bfloat16)
    query_all = query_weight.reshape(AEXP, hpd_count, D, N_HEAD, HD).transpose(0, 2, 3, 1, 4).reshape(AEXP, D, HEADS * HD)
    output_all = output_weight.reshape(AEXP, hpd_count, N_HEAD, HD, D).transpose(0, 2, 1, 3, 4).reshape(AEXP, HEADS * HD, D)
    raw_query = jnp.zeros((REQS, TOPK, HEADS, HD), jnp.bfloat16)
    for expert in range(AEXP):
        projected = jnp.dot(normed, query_all[expert], preferred_element_type=jnp.float32).astype(jnp.bfloat16).reshape(REQS, 1, HEADS, HD)
        raw_query = jnp.where((expert_choice == expert)[:, :, None, None], projected, raw_query)
    query = rotate(raw_query.astype(jnp.float32), cache_length[:, None, None]).astype(jnp.bfloat16)
    score_scale = 1.0 / HD ** 0.5
    positions = jnp.arange(MAXP * PAGE, dtype=jnp.int32)

    def attend(request_item):
        query_row, table_row, length, key_row, value_row = request_item
        keys = cache_keys[table_row].reshape(MAXP * PAGE, HEADS, HD).astype(jnp.float32)
        values = cache_values[table_row].reshape(MAXP * PAGE, HEADS, HD).astype(jnp.float32)
        query_float = query_row.astype(jnp.float32)
        scores = jnp.einsum('khd,thd->kht', query_float, keys, precision=lax.Precision.HIGHEST) * score_scale
        scores = jnp.where((positions < length)[None, None, :], scores, -jnp.inf)
        fresh_score = jnp.einsum('khd,hd->kh', query_float, key_row.astype(jnp.float32), precision=lax.Precision.HIGHEST) * score_scale
        row_top = jnp.maximum(lax.optimization_barrier(jnp.max(scores, axis=2)), fresh_score)
        weights = jnp.exp(scores - row_top[..., None])
        fresh_weight = jnp.exp(fresh_score - row_top)
        denominator = lax.optimization_barrier(jnp.sum(weights, axis=2)) + fresh_weight
        rounded = lax.optimization_barrier(weights.astype(jnp.bfloat16)).astype(jnp.float32)
        fresh_rounded = lax.optimization_barrier(fresh_weight.astype(jnp.bfloat16)).astype(jnp.float32)
        accumulated = jnp.einsum('kht,thd->khd', rounded, values, precision=lax.Precision.HIGHEST)
        accumulated = accumulated + fresh_rounded[..., None] * value_row.astype(jnp.float32)[None]
        return (accumulated / denominator[..., None]).astype(jnp.bfloat16)
    context = lax.map(attend, (query, page_table, cache_length, key_new, value_new))
    result = jnp.zeros((REQS, D), jnp.float32)
    for expert in range(AEXP):
        chosen = expert_choice == expert
        picked = lax.optimization_barrier(jnp.sum(jnp.where(chosen[:, :, None, None], context, jnp.zeros_like(context)), axis=1))
        expert_weight = lax.optimization_barrier(jnp.sum(jnp.where(chosen, expert_gate, jnp.float32(0.0)), axis=1))
        projected = jnp.dot(picked.reshape(REQS, HEADS * HD), output_all[expert], preferred_element_type=jnp.float32)
        result = result + expert_weight[:, None] * projected
    result = result * live_mask.astype(jnp.float32)[:, None]
    return result.astype(jnp.bfloat16)
```

```python
import jax
import jax.numpy as jnp
from jax import lax
from jax.sharding import PartitionSpec as P

AEXP = 8
CAP = 12


eps = 1e-06
theta = 10000.0


def rotate(vectors, positions):
    half_width = vectors.shape[-1] // 2
    frequency = theta ** (-(jnp.arange(half_width, dtype=jnp.float32) * 2.0) / vectors.shape[-1])
    angles = positions.astype(jnp.float32)[..., None] * frequency
    cosine = jnp.cos(angles)
    sine_part = jnp.sin(angles)
    first_half = vectors[..., :half_width]
    second = vectors[..., half_width:]
    return jnp.concatenate(
        [first_half * cosine - second * sine_part, second * cosine + first_half * sine_part],
        axis=-1,
    )


def body(
    tokens,
    norm_gain,
    key_value_weight,
    query_weight,
    output_weight,
    cache_keys,
    cache_values,
    cache_length,
    page_table,
    expert_choice,
    expert_gate,
    live_mask,
):
    groups = lax.axis_size("req")
    group_index = lax.axis_index("req")
    row_count = tokens.shape[0]
    model_width = tokens.shape[1]
    choices_each = expert_choice.shape[1]
    heads_here = key_value_weight.shape[1]
    head_dim = key_value_weight.shape[3]
    pairs_here = query_weight.shape[0]
    pages_here = cache_keys.shape[0]
    page_len = cache_keys.shape[1]
    max_pages = page_table.shape[1]
    experts = AEXP
    capacity = CAP
    as_float = tokens.astype(jnp.float32)
    normed = (
        as_float
        * lax.rsqrt(jnp.mean(as_float * as_float, axis=-1, keepdims=True) + eps)
        * norm_gain
    ).astype(jnp.bfloat16)
    flat_expert = expert_choice.reshape(-1)
    onehot = (flat_expert[:, None] == jnp.arange(experts)[None, :]).astype(jnp.int32)
    before = jnp.cumsum(onehot, axis=0) - onehot
    slot_index = jnp.sum(before * onehot, axis=1)
    target = flat_expert * capacity + slot_index
    select = target[None, :] == jnp.arange(experts * capacity)[:, None]
    select_rows = select.astype(jnp.bfloat16)
    repeated = jnp.repeat(normed, choices_each, axis=0)
    sendbuf = jnp.dot(select_rows, repeated, preferred_element_type=jnp.float32).astype(
        jnp.bfloat16
    )
    replicas = groups // experts
    sendbuf = jnp.broadcast_to(
        sendbuf.reshape(experts, 1, capacity, model_width),
        (experts, replicas, capacity, model_width),
    )
    sendbuf = sendbuf.reshape(groups, capacity, model_width)
    queries_far = jnp.einsum(
        "snd,pdh->spnh",
        lax.all_to_all(sendbuf, "req", split_axis=0, concat_axis=0, tiled=True),
        query_weight,
        preferred_element_type=jnp.float32,
    ).astype(jnp.bfloat16)
    key_value = jnp.einsum(
        "rf,fhkd->rhkd", normed, key_value_weight, preferred_element_type=jnp.float32
    )
    key_new = rotate(key_value[:, :, 0], cache_length[:, None]).astype(jnp.bfloat16)
    value_new = key_value[:, :, 1].astype(jnp.bfloat16)
    local_ids = page_table - group_index * pages_here
    page_used = jnp.arange(max_pages)[None, :] * page_len < cache_length[:, None]
    page_match = page_used[:, :, None] & (
        local_ids[:, :, None] == jnp.arange(pages_here)[None, None, :]
    )
    owned_pages = jnp.any(page_match, axis=1)
    page_taken = jnp.any(owned_pages, axis=0)
    page_owner = jnp.sum(
        owned_pages.astype(jnp.int32) * jnp.arange(row_count, dtype=jnp.int32)[:, None], axis=0
    )
    page_start = jnp.sum(
        page_match.astype(jnp.int32)
        * (jnp.arange(max_pages, dtype=jnp.int32) * page_len)[None, :, None],
        axis=(0, 1),
    )
    page_limit = cache_length[page_owner]
    in_range = page_taken[:, None] & (
        page_start[:, None] + jnp.arange(page_len)[None, :] < page_limit[:, None]
    )
    queries = lax.all_to_all(queries_far, "req", split_axis=0, concat_axis=0, tiled=True)
    queries = (
        queries.reshape(experts, heads_here, capacity, head_dim)
        .transpose(0, 2, 1, 3)
        .reshape(experts * capacity, heads_here, head_dim)
    )
    raw_query = queries[target].reshape(row_count, choices_each, heads_here, head_dim)
    query_rot = rotate(raw_query.astype(jnp.float32), cache_length[:, None, None]).astype(
        jnp.bfloat16
    )
    score_scale = 1.0 / head_dim**0.5
    page_queries = query_rot[page_owner]
    scores = (
        jnp.einsum("pkhd,pthd->pkht", page_queries, cache_keys, preferred_element_type=jnp.float32)
        * score_scale
    )
    scores = jnp.where(in_range[:, None, None, :], scores, -jnp.inf)
    fresh_score = (
        jnp.einsum("rkhd,rhd->rkh", query_rot, key_new, preferred_element_type=jnp.float32)
        * score_scale
    )
    page_top = jnp.max(scores, axis=3)
    owned_top = jnp.max(jnp.where(owned_pages[:, :, None, None], page_top[None], -jnp.inf), axis=1)
    row_top = jnp.maximum(owned_top, fresh_score)
    weights = jnp.exp(scores - row_top[page_owner][..., None])
    fresh_weight = jnp.exp(fresh_score - row_top)
    owned_float = owned_pages.astype(jnp.float32)
    denominator = (
        jnp.einsum(
            "rp,pkh->rkh", owned_float, jnp.sum(weights, axis=3), precision=lax.Precision.HIGHEST
        )
        + fresh_weight
    )
    weights_rounded = weights.astype(jnp.bfloat16)
    fresh_rounded = lax.optimization_barrier(fresh_weight.astype(jnp.bfloat16)).astype(jnp.float32)
    page_context = jnp.einsum(
        "pkht,pthd->pkhd", weights_rounded, cache_values, preferred_element_type=jnp.float32
    )
    accumulated = jnp.einsum(
        "rp,pkhd->rkhd", owned_float, page_context, precision=lax.Precision.HIGHEST
    )
    accumulated = accumulated + fresh_rounded[..., None] * value_new.astype(jnp.float32)[:, None]
    context = (accumulated / denominator[..., None]).astype(jnp.bfloat16)
    context_flat = context.reshape(row_count * choices_each, heads_here * head_dim)
    context_buf = jnp.dot(select_rows, context_flat, preferred_element_type=jnp.float32).astype(
        jnp.bfloat16
    )
    context_buf = context_buf.reshape(experts, capacity, heads_here, head_dim).transpose(0, 2, 1, 3)
    context_buf = context_buf.reshape(groups, pairs_here, capacity, head_dim)
    partial_far = jnp.einsum(
        "spnh,phd->snd",
        lax.all_to_all(context_buf, "req", split_axis=0, concat_axis=0, tiled=True),
        output_weight,
        preferred_element_type=jnp.float32,
    )
    gate_flat = expert_gate.reshape(-1)
    spread = (
        jnp.where(select, gate_flat[None, :], jnp.float32(0.0))
        .reshape(experts * capacity, row_count, choices_each)
        .sum(axis=2)
        .T
    )
    alive_rows = live_mask.astype(jnp.float32)[:, None]
    returned = lax.all_to_all(partial_far, "req", split_axis=0, concat_axis=0, tiled=True)
    summed = returned.reshape(experts, replicas, capacity, model_width).sum(axis=1)
    own_sum = jnp.dot(
        spread, summed.reshape(experts * capacity, model_width), precision=lax.Precision.HIGHEST
    )
    result = lax.psum_scatter(own_sum, "head", scatter_dimension=1, tiled=True)
    return (result * alive_rows).astype(jnp.bfloat16)


def solution(mesh):
    return jax.shard_map(
        body,
        mesh=mesh,
        in_specs=(
            P("req", None),
            P(),
            P(None, "head", None, None),
            P("req", None, "head"),
            P("req", "head", None),
            P("req", None, "head", None),
            P("req", None, "head", None),
            P("req"),
            P("req", None),
            P("req", None),
            P("req", None),
            P("req"),
        ),
        out_specs=P("req", "head"),
        check_vma=False,
    )
```

```python
import jax
import jax.numpy as jnp
from jax import lax
from jax.sharding import PartitionSpec as P

AEXP = 8
CAP = 12


eps = 1e-06
theta = 10000.0


def rotate(vectors, positions):
    half_width = vectors.shape[-1] // 2
    frequency = theta ** (-(jnp.arange(half_width, dtype=jnp.float32) * 2.0) / vectors.shape[-1])
    angles = positions.astype(jnp.float32)[..., None] * frequency
    cosine = jnp.cos(angles)
    sine_part = jnp.sin(angles)
    first_half = vectors[..., :half_width]
    second = vectors[..., half_width:]
    return jnp.concatenate(
        [first_half * cosine - second * sine_part, second * cosine + first_half * sine_part],
        axis=-1,
    )


def body(
    tokens,
    norm_gain,
    key_value_weight,
    query_weight,
    output_weight,
    cache_keys,
    cache_values,
    cache_length,
    page_table,
    expert_choice,
    expert_gate,
    live_mask,
):
    groups = lax.axis_size("req")
    group_index = lax.axis_index("req")
    row_count = tokens.shape[0]
    model_width = tokens.shape[1]
    choices_each = expert_choice.shape[1]
    heads_here = key_value_weight.shape[1]
    head_dim = key_value_weight.shape[3]
    pairs_here = query_weight.shape[0]
    pages_here = cache_keys.shape[0]
    page_len = cache_keys.shape[1]
    max_pages = page_table.shape[1]
    experts = AEXP
    capacity = CAP
    as_float = tokens.astype(jnp.float32)
    normed = (
        as_float
        * lax.rsqrt(jnp.mean(as_float * as_float, axis=-1, keepdims=True) + eps)
        * norm_gain
    ).astype(jnp.bfloat16)
    flat_expert = expert_choice.reshape(-1)
    onehot = (flat_expert[:, None] == jnp.arange(experts)[None, :]).astype(jnp.int32)
    before = jnp.cumsum(onehot, axis=0) - onehot
    slot_index = jnp.sum(before * onehot, axis=1)
    target = flat_expert * capacity + slot_index
    select = target[None, :] == jnp.arange(experts * capacity)[:, None]
    select_rows = select.astype(jnp.bfloat16)
    repeated = jnp.repeat(normed, choices_each, axis=0)
    sendbuf = jnp.dot(select_rows, repeated, preferred_element_type=jnp.float32).astype(
        jnp.bfloat16
    )
    replicas = groups // experts
    sendbuf = jnp.broadcast_to(
        sendbuf.reshape(experts, 1, capacity, model_width),
        (experts, replicas, capacity, model_width),
    )
    sendbuf = sendbuf.reshape(groups, capacity, model_width)
    queries_far = jnp.einsum(
        "snd,pdh->spnh",
        lax.all_to_all(sendbuf, "req", split_axis=0, concat_axis=0, tiled=True),
        query_weight,
        preferred_element_type=jnp.float32,
    ).astype(jnp.bfloat16)
    key_value = jnp.einsum(
        "rf,fhkd->rhkd", normed, key_value_weight, preferred_element_type=jnp.float32
    )
    key_new = rotate(key_value[:, :, 0], cache_length[:, None]).astype(jnp.bfloat16)
    value_new = key_value[:, :, 1].astype(jnp.bfloat16)
    local_ids = page_table - group_index * pages_here
    page_used = jnp.arange(max_pages)[None, :] * page_len < cache_length[:, None]
    page_match = page_used[:, :, None] & (
        local_ids[:, :, None] == jnp.arange(pages_here)[None, None, :]
    )
    owned_pages = jnp.any(page_match, axis=1)
    page_taken = jnp.any(owned_pages, axis=0)
    page_owner = jnp.sum(
        owned_pages.astype(jnp.int32) * jnp.arange(row_count, dtype=jnp.int32)[:, None], axis=0
    )
    page_start = jnp.sum(
        page_match.astype(jnp.int32)
        * (jnp.arange(max_pages, dtype=jnp.int32) * page_len)[None, :, None],
        axis=(0, 1),
    )
    page_limit = cache_length[page_owner]
    in_range = page_taken[:, None] & (
        page_start[:, None] + jnp.arange(page_len)[None, :] < page_limit[:, None]
    )
    queries = lax.all_to_all(queries_far, "req", split_axis=0, concat_axis=0, tiled=True)
    queries = (
        queries.reshape(experts, heads_here, capacity, head_dim)
        .transpose(0, 2, 1, 3)
        .reshape(experts * capacity, heads_here, head_dim)
    )
    raw_query = queries[target].reshape(row_count, choices_each, heads_here, head_dim)
    query_rot = rotate(raw_query.astype(jnp.float32), cache_length[:, None, None]).astype(
        jnp.bfloat16
    )
    score_scale = 1.0 / head_dim**0.5
    page_queries = query_rot[page_owner]
    scores = (
        jnp.einsum("pkhd,pthd->pkht", page_queries, cache_keys, preferred_element_type=jnp.float32)
        * score_scale
    )
    scores = jnp.where(in_range[:, None, None, :], scores, -jnp.inf)
    fresh_score = (
        jnp.einsum("rkhd,rhd->rkh", query_rot, key_new, preferred_element_type=jnp.float32)
        * score_scale
    )
    page_top = jnp.max(scores, axis=3)
    owned_top = jnp.max(jnp.where(owned_pages[:, :, None, None], page_top[None], -jnp.inf), axis=1)
    row_top = jnp.maximum(owned_top, fresh_score)
    weights = jnp.exp(scores - row_top[page_owner][..., None])
    fresh_weight = jnp.exp(fresh_score - row_top)
    owned_float = owned_pages.astype(jnp.float32)
    denominator = (
        jnp.einsum(
            "rp,pkh->rkh", owned_float, jnp.sum(weights, axis=3), precision=lax.Precision.HIGHEST
        )
        + fresh_weight
    )
    weights_rounded = weights.astype(jnp.bfloat16)
    fresh_rounded = lax.optimization_barrier(fresh_weight.astype(jnp.bfloat16)).astype(jnp.float32)
    page_context = jnp.einsum(
        "pkht,pthd->pkhd", weights_rounded, cache_values, preferred_element_type=jnp.float32
    )
    accumulated = jnp.einsum(
        "rp,pkhd->rkhd", owned_float, page_context, precision=lax.Precision.HIGHEST
    )
    accumulated = accumulated + fresh_rounded[..., None] * value_new.astype(jnp.float32)[:, None]
    context = (accumulated / denominator[..., None]).astype(jnp.bfloat16)
    context_flat = context.reshape(row_count * choices_each, heads_here * head_dim)
    context_buf = jnp.dot(select_rows, context_flat, preferred_element_type=jnp.float32).astype(
        jnp.bfloat16
    )
    context_buf = context_buf.reshape(experts, capacity, heads_here, head_dim).transpose(0, 2, 1, 3)
    context_buf = context_buf.reshape(groups, pairs_here, capacity, head_dim)
    partial_far = jnp.einsum(
        "spnh,phd->snd",
        lax.all_to_all(context_buf, "req", split_axis=0, concat_axis=0, tiled=True),
        output_weight,
        preferred_element_type=jnp.float32,
    )
    gate_flat = expert_gate.reshape(-1)
    spread = (
        jnp.where(select, gate_flat[None, :], jnp.float32(0.0))
        .reshape(experts * capacity, row_count, choices_each)
        .sum(axis=2)
        .T
    )
    alive_rows = live_mask.astype(jnp.float32)[:, None]
    head_count = lax.axis_size("head")
    width_here = model_width // head_count
    partial_far = partial_far.reshape(groups, capacity, head_count, width_here).transpose(0, 2, 1, 3)
    returned = lax.all_to_all(
        partial_far.reshape(groups * head_count, capacity, width_here),
        ("req", "head"),
        split_axis=0,
        concat_axis=0,
        tiled=True,
    )
    summed = returned.reshape(experts, replicas * head_count, capacity, width_here).sum(axis=1)
    result = jnp.dot(
        spread, summed.reshape(experts * capacity, width_here), precision=lax.Precision.HIGHEST
    )
    return (result * alive_rows).astype(jnp.bfloat16)


def solution(mesh):
    return jax.shard_map(
        body,
        mesh=mesh,
        in_specs=(
            P("req", None),
            P(),
            P(None, "head", None, None),
            P("req", None, "head"),
            P("req", "head", None),
            P("req", None, "head", None),
            P("req", None, "head", None),
            P("req"),
            P("req", None),
            P("req", None),
            P("req", None),
            P("req"),
        ),
        out_specs=P("req", "head"),
        check_vma=False,
    )
```

```python
import jax
import jax.numpy as jnp
from jax import lax
from jax.sharding import PartitionSpec as P

AEXP = 8
CAP = 12


eps = 1e-06
theta = 10000.0


def rotate(vectors, positions):
    half_width = vectors.shape[-1] // 2
    frequency = theta ** (-(jnp.arange(half_width, dtype=jnp.float32) * 2.0) / vectors.shape[-1])
    angles = positions.astype(jnp.float32)[..., None] * frequency
    cosine = jnp.cos(angles)
    sine_part = jnp.sin(angles)
    first_half = vectors[..., :half_width]
    second = vectors[..., half_width:]
    return jnp.concatenate(
        [first_half * cosine - second * sine_part, second * cosine + first_half * sine_part],
        axis=-1,
    )


def body(
    tokens,
    norm_gain,
    key_value_weight,
    query_weight,
    output_weight,
    cache_keys,
    cache_values,
    cache_length,
    page_table,
    expert_choice,
    expert_gate,
    live_mask,
):
    groups = lax.axis_size("req")
    group_index = lax.axis_index("req")
    row_count = tokens.shape[0]
    model_width = tokens.shape[1]
    choices_each = expert_choice.shape[1]
    heads_here = key_value_weight.shape[1]
    head_dim = key_value_weight.shape[3]
    pairs_here = query_weight.shape[0]
    pages_here = cache_keys.shape[0]
    page_len = cache_keys.shape[1]
    max_pages = page_table.shape[1]
    experts = AEXP
    capacity = CAP
    as_float = tokens.astype(jnp.float32)
    normed = (
        as_float
        * lax.rsqrt(jnp.mean(as_float * as_float, axis=-1, keepdims=True) + eps)
        * norm_gain
    ).astype(jnp.bfloat16)
    flat_expert = expert_choice.reshape(-1)
    onehot = (flat_expert[:, None] == jnp.arange(experts)[None, :]).astype(jnp.int32)
    before = jnp.cumsum(onehot, axis=0) - onehot
    slot_index = jnp.sum(before * onehot, axis=1)
    target = flat_expert * capacity + slot_index
    select = target[None, :] == jnp.arange(experts * capacity)[:, None]
    select_rows = select.astype(jnp.bfloat16)
    repeated = jnp.repeat(normed, choices_each, axis=0)
    sendbuf = jnp.dot(select_rows, repeated, preferred_element_type=jnp.float32).astype(
        jnp.bfloat16
    )
    replicas = groups // experts
    sendbuf = jnp.broadcast_to(
        sendbuf.reshape(experts, 1, capacity, model_width),
        (experts, replicas, capacity, model_width),
    )
    sendbuf = sendbuf.reshape(groups, capacity, model_width)
    queries_far = jnp.einsum(
        "snd,pdh->spnh",
        lax.all_to_all(sendbuf, "req", split_axis=0, concat_axis=0, tiled=True),
        query_weight,
        preferred_element_type=jnp.float32,
    ).astype(jnp.bfloat16)
    key_value = jnp.einsum(
        "rf,fhkd->rhkd", normed, key_value_weight, preferred_element_type=jnp.float32
    )
    key_new = rotate(key_value[:, :, 0], cache_length[:, None]).astype(jnp.bfloat16)
    value_new = key_value[:, :, 1].astype(jnp.bfloat16)
    local_ids = page_table - group_index * pages_here
    page_used = jnp.arange(max_pages)[None, :] * page_len < cache_length[:, None]
    page_match = page_used[:, :, None] & (
        local_ids[:, :, None] == jnp.arange(pages_here)[None, None, :]
    )
    owned_pages = jnp.any(page_match, axis=1)
    page_taken = jnp.any(owned_pages, axis=0)
    page_owner = jnp.sum(
        owned_pages.astype(jnp.int32) * jnp.arange(row_count, dtype=jnp.int32)[:, None], axis=0
    )
    page_start = jnp.sum(
        page_match.astype(jnp.int32)
        * (jnp.arange(max_pages, dtype=jnp.int32) * page_len)[None, :, None],
        axis=(0, 1),
    )
    page_limit = cache_length[page_owner]
    in_range = page_taken[:, None] & (
        page_start[:, None] + jnp.arange(page_len)[None, :] < page_limit[:, None]
    )
    queries = lax.all_to_all(queries_far, "req", split_axis=0, concat_axis=0, tiled=True)
    queries = (
        queries.reshape(experts, heads_here, capacity, head_dim)
        .transpose(0, 2, 1, 3)
        .reshape(experts * capacity, heads_here, head_dim)
    )
    raw_query = queries[target].reshape(row_count, choices_each, heads_here, head_dim)
    query_rot = rotate(raw_query.astype(jnp.float32), cache_length[:, None, None]).astype(
        jnp.bfloat16
    )
    score_scale = 1.0 / head_dim**0.5
    page_queries = query_rot[page_owner]
    scores = (
        jnp.einsum("pkhd,pthd->pkht", page_queries, cache_keys, preferred_element_type=jnp.float32)
        * score_scale
    )
    scores = jnp.where(in_range[:, None, None, :], scores, -jnp.inf)
    fresh_score = (
        jnp.einsum("rkhd,rhd->rkh", query_rot, key_new, preferred_element_type=jnp.float32)
        * score_scale
    )
    page_top = jnp.max(scores, axis=3)
    owned_top = jnp.max(jnp.where(owned_pages[:, :, None, None], page_top[None], -jnp.inf), axis=1)
    row_top = jnp.maximum(owned_top, fresh_score)
    weights = jnp.exp(scores - row_top[page_owner][..., None])
    fresh_weight = jnp.exp(fresh_score - row_top)
    owned_float = owned_pages.astype(jnp.float32)
    denominator = (
        jnp.einsum(
            "rp,pkh->rkh", owned_float, jnp.sum(weights, axis=3), precision=lax.Precision.HIGHEST
        )
        + fresh_weight
    )
    weights_rounded = weights.astype(jnp.bfloat16)
    fresh_rounded = lax.optimization_barrier(fresh_weight.astype(jnp.bfloat16)).astype(jnp.float32)
    page_context = jnp.einsum(
        "pkht,pthd->pkhd", weights_rounded, cache_values, preferred_element_type=jnp.float32
    )
    accumulated = jnp.einsum(
        "rp,pkhd->rkhd", owned_float, page_context, precision=lax.Precision.HIGHEST
    )
    accumulated = accumulated + fresh_rounded[..., None] * value_new.astype(jnp.float32)[:, None]
    context = (accumulated / denominator[..., None]).astype(jnp.bfloat16)
    context_flat = context.reshape(row_count * choices_each, heads_here * head_dim)
    context_buf = jnp.dot(select_rows, context_flat, preferred_element_type=jnp.float32).astype(
        jnp.bfloat16
    )
    context_buf = context_buf.reshape(experts, capacity, heads_here, head_dim).transpose(0, 2, 1, 3)
    context_buf = context_buf.reshape(groups, pairs_here, capacity, head_dim)
    partial_far = jnp.einsum(
        "spnh,phd->snd",
        lax.all_to_all(context_buf, "req", split_axis=0, concat_axis=0, tiled=True),
        output_weight,
        preferred_element_type=jnp.float32,
    )
    gate_flat = expert_gate.reshape(-1)
    spread = (
        jnp.where(select, gate_flat[None, :], jnp.float32(0.0))
        .reshape(experts * capacity, row_count, choices_each)
        .sum(axis=2)
        .T
    )
    alive_rows = live_mask.astype(jnp.float32)[:, None]
    head_count = lax.axis_size("head")
    width_here = model_width // head_count
    partial_far = partial_far.reshape(groups, capacity, head_count, width_here).transpose(0, 2, 1, 3)
    returned = lax.all_to_all(
        partial_far.reshape(groups * head_count, capacity, width_here).astype(jnp.bfloat16),
        ("req", "head"),
        split_axis=0,
        concat_axis=0,
        tiled=True,
    )
    summed = (
        returned.astype(jnp.float32)
        .reshape(experts, replicas * head_count, capacity, width_here)
        .sum(axis=1)
    )
    result = jnp.dot(
        spread, summed.reshape(experts * capacity, width_here), precision=lax.Precision.HIGHEST
    )
    return (result * alive_rows).astype(jnp.bfloat16)


def solution(mesh):
    return jax.shard_map(
        body,
        mesh=mesh,
        in_specs=(
            P("req", None),
            P(),
            P(None, "head", None, None),
            P("req", None, "head"),
            P("req", "head", None),
            P("req", None, "head", None),
            P("req", None, "head", None),
            P("req"),
            P("req", None),
            P("req", None),
            P("req", None),
            P("req"),
        ),
        out_specs=P("req", "head"),
        check_vma=False,
    )
```

```python
import jax
import jax.numpy as jnp
from jax import lax
from jax.sharding import PartitionSpec as P

AEXP = 8
CAP = 12
CHUNKS = 2


eps = 1e-06
theta = 10000.0


def rotate(vectors, positions):
    half_width = vectors.shape[-1] // 2
    frequency = theta ** (-(jnp.arange(half_width, dtype=jnp.float32) * 2.0) / vectors.shape[-1])
    angles = positions.astype(jnp.float32)[..., None] * frequency
    cosine = jnp.cos(angles)
    sine_part = jnp.sin(angles)
    first_half = vectors[..., :half_width]
    second = vectors[..., half_width:]
    return jnp.concatenate(
        [first_half * cosine - second * sine_part, second * cosine + first_half * sine_part],
        axis=-1,
    )


def body(
    tokens,
    norm_gain,
    key_value_weight,
    query_weight,
    output_weight,
    cache_keys,
    cache_values,
    cache_length,
    page_table,
    expert_choice,
    expert_gate,
    live_mask,
):
    groups = lax.axis_size("req")
    group_index = lax.axis_index("req")
    row_count = tokens.shape[0]
    model_width = tokens.shape[1]
    choices_each = expert_choice.shape[1]
    heads_here = key_value_weight.shape[1]
    head_dim = key_value_weight.shape[3]
    pairs_here = query_weight.shape[0]
    pages_here = cache_keys.shape[0]
    page_len = cache_keys.shape[1]
    max_pages = page_table.shape[1]
    experts = AEXP
    capacity = CAP
    as_float = tokens.astype(jnp.float32)
    normed = (
        as_float
        * lax.rsqrt(jnp.mean(as_float * as_float, axis=-1, keepdims=True) + eps)
        * norm_gain
    ).astype(jnp.bfloat16)
    flat_expert = expert_choice.reshape(-1)
    onehot = (flat_expert[:, None] == jnp.arange(experts)[None, :]).astype(jnp.int32)
    before = jnp.cumsum(onehot, axis=0) - onehot
    slot_index = jnp.sum(before * onehot, axis=1)
    target = flat_expert * capacity + slot_index
    select = target[None, :] == jnp.arange(experts * capacity)[:, None]
    select_rows = select.astype(jnp.bfloat16)
    repeated = jnp.repeat(normed, choices_each, axis=0)
    sendbuf = jnp.dot(select_rows, repeated, preferred_element_type=jnp.float32).astype(
        jnp.bfloat16
    )
    replicas = groups // experts
    sendbuf = jnp.broadcast_to(
        sendbuf.reshape(experts, 1, capacity, model_width),
        (experts, replicas, capacity, model_width),
    )
    sendbuf = sendbuf.reshape(groups, capacity, model_width)
    tokens_far = lax.all_to_all(sendbuf, "req", split_axis=0, concat_axis=0, tiled=True)
    key_value = jnp.einsum(
        "rf,fhkd->rhkd", normed, key_value_weight, preferred_element_type=jnp.float32
    )
    key_new = rotate(key_value[:, :, 0], cache_length[:, None]).astype(jnp.bfloat16)
    value_new = key_value[:, :, 1].astype(jnp.bfloat16)
    local_ids = page_table - group_index * pages_here
    page_used = jnp.arange(max_pages)[None, :] * page_len < cache_length[:, None]
    page_match = page_used[:, :, None] & (
        local_ids[:, :, None] == jnp.arange(pages_here)[None, None, :]
    )
    owned_pages = jnp.any(page_match, axis=1)
    page_taken = jnp.any(owned_pages, axis=0)
    page_owner = jnp.sum(
        owned_pages.astype(jnp.int32) * jnp.arange(row_count, dtype=jnp.int32)[:, None], axis=0
    )
    page_start = jnp.sum(
        page_match.astype(jnp.int32)
        * (jnp.arange(max_pages, dtype=jnp.int32) * page_len)[None, :, None],
        axis=(0, 1),
    )
    page_limit = cache_length[page_owner]
    in_range = page_taken[:, None] & (
        page_start[:, None] + jnp.arange(page_len)[None, :] < page_limit[:, None]
    )
    score_scale = 1.0 / head_dim**0.5
    owned_float = owned_pages.astype(jnp.float32)
    chunks = CHUNKS if pairs_here % CHUNKS == 0 else 1
    pairs_chunk = pairs_here // chunks
    partial_far = None
    for chunk in range(chunks):
        first = chunk * pairs_chunk
        head_ids = [r * pairs_here + first + i for r in range(replicas) for i in range(pairs_chunk)]
        chunk_heads = len(head_ids)

        def pick(array, axis):
            if head_ids == list(range(head_ids[0], head_ids[0] + chunk_heads)):
                return lax.slice_in_dim(array, head_ids[0], head_ids[0] + chunk_heads, axis=axis)
            return jnp.take(array, jnp.asarray(head_ids), axis=axis)

        queries_far = jnp.einsum(
            "snd,pdh->spnh",
            tokens_far,
            query_weight[first : first + pairs_chunk],
            preferred_element_type=jnp.float32,
        ).astype(jnp.bfloat16)
        queries = lax.all_to_all(queries_far, "req", split_axis=0, concat_axis=0, tiled=True)
        queries = (
            queries.reshape(experts, chunk_heads, capacity, head_dim)
            .transpose(0, 2, 1, 3)
            .reshape(experts * capacity, chunk_heads, head_dim)
        )
        raw_query = queries[target].reshape(row_count, choices_each, chunk_heads, head_dim)
        query_rot = rotate(raw_query.astype(jnp.float32), cache_length[:, None, None]).astype(
            jnp.bfloat16
        )
        keys_here = pick(cache_keys, 2)
        values_here = pick(cache_values, 2)
        key_chunk = pick(key_new, 1)
        value_chunk = pick(value_new, 1)
        page_queries = query_rot[page_owner]
        scores = (
            jnp.einsum(
                "pkhd,pthd->pkht", page_queries, keys_here, preferred_element_type=jnp.float32
            )
            * score_scale
        )
        scores = jnp.where(in_range[:, None, None, :], scores, -jnp.inf)
        fresh_score = (
            jnp.einsum("rkhd,rhd->rkh", query_rot, key_chunk, preferred_element_type=jnp.float32)
            * score_scale
        )
        page_top = jnp.max(scores, axis=3)
        owned_top = jnp.max(
            jnp.where(owned_pages[:, :, None, None], page_top[None], -jnp.inf), axis=1
        )
        row_top = jnp.maximum(owned_top, fresh_score)
        weights = jnp.exp(scores - row_top[page_owner][..., None])
        fresh_weight = jnp.exp(fresh_score - row_top)
        denominator = (
            jnp.einsum(
                "rp,pkh->rkh",
                owned_float,
                jnp.sum(weights, axis=3),
                precision=lax.Precision.HIGHEST,
            )
            + fresh_weight
        )
        weights_rounded = weights.astype(jnp.bfloat16)
        fresh_rounded = lax.optimization_barrier(fresh_weight.astype(jnp.bfloat16)).astype(
            jnp.float32
        )
        page_context = jnp.einsum(
            "pkht,pthd->pkhd", weights_rounded, values_here, preferred_element_type=jnp.float32
        )
        accumulated = jnp.einsum(
            "rp,pkhd->rkhd", owned_float, page_context, precision=lax.Precision.HIGHEST
        )
        accumulated = (
            accumulated + fresh_rounded[..., None] * value_chunk.astype(jnp.float32)[:, None]
        )
        context = (accumulated / denominator[..., None]).astype(jnp.bfloat16)
        context_flat = context.reshape(row_count * choices_each, chunk_heads * head_dim)
        context_buf = jnp.dot(
            select_rows, context_flat, preferred_element_type=jnp.float32
        ).astype(jnp.bfloat16)
        context_buf = context_buf.reshape(
            experts, capacity, replicas, pairs_chunk, head_dim
        ).transpose(0, 2, 3, 1, 4)
        context_buf = context_buf.reshape(groups, pairs_chunk, capacity, head_dim)
        chunk_partial = jnp.einsum(
            "spnh,phd->snd",
            lax.all_to_all(context_buf, "req", split_axis=0, concat_axis=0, tiled=True),
            output_weight[first : first + pairs_chunk],
            preferred_element_type=jnp.float32,
        )
        partial_far = chunk_partial if partial_far is None else partial_far + chunk_partial
    gate_flat = expert_gate.reshape(-1)
    spread = (
        jnp.where(select, gate_flat[None, :], jnp.float32(0.0))
        .reshape(experts * capacity, row_count, choices_each)
        .sum(axis=2)
        .T
    )
    alive_rows = live_mask.astype(jnp.float32)[:, None]
    head_count = lax.axis_size("head")
    width_here = model_width // head_count
    partial_far = partial_far.reshape(groups, capacity, head_count, width_here).transpose(0, 2, 1, 3)
    returned = lax.all_to_all(
        partial_far.reshape(groups * head_count, capacity, width_here),
        ("req", "head"),
        split_axis=0,
        concat_axis=0,
        tiled=True,
    )
    summed = returned.reshape(experts, replicas * head_count, capacity, width_here).sum(axis=1)
    result = jnp.dot(
        spread, summed.reshape(experts * capacity, width_here), precision=lax.Precision.HIGHEST
    )
    return (result * alive_rows).astype(jnp.bfloat16)


def solution(mesh):
    return jax.shard_map(
        body,
        mesh=mesh,
        in_specs=(
            P("req", None),
            P(),
            P(None, "head", None, None),
            P("req", None, "head"),
            P("req", "head", None),
            P("req", None, "head", None),
            P("req", None, "head", None),
            P("req"),
            P("req", None),
            P("req", None),
            P("req", None),
            P("req"),
        ),
        out_specs=P("req", "head"),
        check_vma=False,
    )
```

```python
import jax
import jax.numpy as jnp
from jax import lax
from jax.sharding import PartitionSpec as P

AEXP = 8
CAP = 12


eps = 1e-06
theta = 10000.0


def rotate(vectors, positions):
    half_width = vectors.shape[-1] // 2
    frequency = theta ** (-(jnp.arange(half_width, dtype=jnp.float32) * 2.0) / vectors.shape[-1])
    angles = positions.astype(jnp.float32)[..., None] * frequency
    cosine = jnp.cos(angles)
    sine_part = jnp.sin(angles)
    first_half = vectors[..., :half_width]
    second = vectors[..., half_width:]
    return jnp.concatenate(
        [first_half * cosine - second * sine_part, second * cosine + first_half * sine_part],
        axis=-1,
    )


def body(
    tokens,
    norm_gain,
    key_value_weight,
    query_weight,
    output_weight,
    cache_keys,
    cache_values,
    cache_length,
    page_table,
    expert_choice,
    expert_gate,
    live_mask,
):
    groups = lax.axis_size("req")
    group_index = lax.axis_index("req")
    row_count = tokens.shape[0]
    model_width = tokens.shape[1]
    choices_each = expert_choice.shape[1]
    heads_here = key_value_weight.shape[1]
    head_dim = key_value_weight.shape[3]
    pairs_here = query_weight.shape[0]
    pages_here = cache_keys.shape[0]
    page_len = cache_keys.shape[1]
    max_pages = page_table.shape[1]
    experts = AEXP
    capacity = CAP
    as_float = tokens.astype(jnp.float32)
    normed = (
        as_float
        * lax.rsqrt(jnp.mean(as_float * as_float, axis=-1, keepdims=True) + eps)
        * norm_gain
    ).astype(jnp.bfloat16)
    flat_expert = expert_choice.reshape(-1)
    onehot = (flat_expert[:, None] == jnp.arange(experts)[None, :]).astype(jnp.int32)
    before = jnp.cumsum(onehot, axis=0) - onehot
    slot_index = jnp.sum(before * onehot, axis=1)
    target = flat_expert * capacity + slot_index
    select = target[None, :] == jnp.arange(experts * capacity)[:, None]
    select_rows = select.astype(jnp.bfloat16)
    repeated = jnp.repeat(normed, choices_each, axis=0)
    sendbuf = jnp.dot(select_rows, repeated, preferred_element_type=jnp.float32).astype(
        jnp.bfloat16
    )
    replicas = groups // experts
    sendbuf = jnp.broadcast_to(
        sendbuf.reshape(experts, 1, capacity, model_width),
        (experts, replicas, capacity, model_width),
    )
    sendbuf = sendbuf.reshape(groups, capacity, model_width)
    queries_far = jnp.einsum(
        "snd,pdh->spnh",
        lax.all_to_all(sendbuf, "req", split_axis=0, concat_axis=0, tiled=True),
        query_weight,
        preferred_element_type=jnp.float32,
    ).astype(jnp.bfloat16)
    key_value = jnp.einsum(
        "rf,fhkd->rhkd", normed, key_value_weight, preferred_element_type=jnp.float32
    )
    key_new = rotate(key_value[:, :, 0], cache_length[:, None]).astype(jnp.bfloat16)
    value_new = key_value[:, :, 1].astype(jnp.bfloat16)
    local_ids = page_table - group_index * pages_here
    page_used = jnp.arange(max_pages)[None, :] * page_len < cache_length[:, None]
    page_match = page_used[:, :, None] & (
        local_ids[:, :, None] == jnp.arange(pages_here)[None, None, :]
    )
    owned_pages = jnp.any(page_match, axis=1)
    page_taken = jnp.any(owned_pages, axis=0)
    page_owner = jnp.sum(
        owned_pages.astype(jnp.int32) * jnp.arange(row_count, dtype=jnp.int32)[:, None], axis=0
    )
    page_start = jnp.sum(
        page_match.astype(jnp.int32)
        * (jnp.arange(max_pages, dtype=jnp.int32) * page_len)[None, :, None],
        axis=(0, 1),
    )
    page_limit = cache_length[page_owner]
    in_range = page_taken[:, None] & (
        page_start[:, None] + jnp.arange(page_len)[None, :] < page_limit[:, None]
    )
    queries = lax.all_to_all(queries_far, "req", split_axis=0, concat_axis=0, tiled=True)
    queries = (
        queries.reshape(experts, heads_here, capacity, head_dim)
        .transpose(0, 2, 1, 3)
        .reshape(experts * capacity, heads_here, head_dim)
    )
    raw_query = queries[target].reshape(row_count, choices_each, heads_here, head_dim)
    query_rot = rotate(raw_query.astype(jnp.float32), cache_length[:, None, None]).astype(
        jnp.bfloat16
    )
    score_scale = 1.0 / head_dim**0.5
    page_queries = query_rot[page_owner]
    head_eye = jnp.eye(heads_here, dtype=jnp.bfloat16)
    spread_queries = page_queries[:, :, :, None, :] * head_eye[None, None, :, :, None]
    scores = (
        jnp.einsum(
            "pkjhd,pthd->pkjt", spread_queries, cache_keys, preferred_element_type=jnp.float32
        )
        * score_scale
    )
    scores = jnp.where(in_range[:, None, None, :], scores, -jnp.inf)
    fresh_score = (
        jnp.einsum("rkhd,rhd->rkh", query_rot, key_new, preferred_element_type=jnp.float32)
        * score_scale
    )
    page_top = jnp.max(scores, axis=3)
    owned_top = jnp.max(jnp.where(owned_pages[:, :, None, None], page_top[None], -jnp.inf), axis=1)
    row_top = jnp.maximum(owned_top, fresh_score)
    weights = jnp.exp(scores - row_top[page_owner][..., None])
    fresh_weight = jnp.exp(fresh_score - row_top)
    owned_float = owned_pages.astype(jnp.float32)
    denominator = (
        jnp.einsum(
            "rp,pkh->rkh", owned_float, jnp.sum(weights, axis=3), precision=lax.Precision.HIGHEST
        )
        + fresh_weight
    )
    weights_rounded = weights.astype(jnp.bfloat16)
    fresh_rounded = lax.optimization_barrier(fresh_weight.astype(jnp.bfloat16)).astype(jnp.float32)
    page_context = jnp.einsum(
        "pkjt,pthd->pkjhd", weights_rounded, cache_values, preferred_element_type=jnp.float32
    )
    page_context = jnp.sum(page_context * head_eye.astype(jnp.float32)[None, None, :, :, None], axis=3)
    accumulated = jnp.einsum(
        "rp,pkhd->rkhd", owned_float, page_context, precision=lax.Precision.HIGHEST
    )
    accumulated = accumulated + fresh_rounded[..., None] * value_new.astype(jnp.float32)[:, None]
    context = (accumulated / denominator[..., None]).astype(jnp.bfloat16)
    context_flat = context.reshape(row_count * choices_each, heads_here * head_dim)
    context_buf = jnp.dot(select_rows, context_flat, preferred_element_type=jnp.float32).astype(
        jnp.bfloat16
    )
    context_buf = context_buf.reshape(experts, capacity, heads_here, head_dim).transpose(0, 2, 1, 3)
    context_buf = context_buf.reshape(groups, pairs_here, capacity, head_dim)
    partial_far = jnp.einsum(
        "spnh,phd->snd",
        lax.all_to_all(context_buf, "req", split_axis=0, concat_axis=0, tiled=True),
        output_weight,
        preferred_element_type=jnp.float32,
    )
    gate_flat = expert_gate.reshape(-1)
    spread = (
        jnp.where(select, gate_flat[None, :], jnp.float32(0.0))
        .reshape(experts * capacity, row_count, choices_each)
        .sum(axis=2)
        .T
    )
    alive_rows = live_mask.astype(jnp.float32)[:, None]
    head_count = lax.axis_size("head")
    width_here = model_width // head_count
    partial_far = partial_far.reshape(groups, capacity, head_count, width_here).transpose(0, 2, 1, 3)
    returned = lax.all_to_all(
        partial_far.reshape(groups * head_count, capacity, width_here),
        ("req", "head"),
        split_axis=0,
        concat_axis=0,
        tiled=True,
    )
    summed = returned.reshape(experts, replicas * head_count, capacity, width_here).sum(axis=1)
    result = jnp.dot(
        spread, summed.reshape(experts * capacity, width_here), precision=lax.Precision.HIGHEST
    )
    return (result * alive_rows).astype(jnp.bfloat16)


def solution(mesh):
    return jax.shard_map(
        body,
        mesh=mesh,
        in_specs=(
            P("req", None),
            P(),
            P(None, "head", None, None),
            P("req", None, "head"),
            P("req", "head", None),
            P("req", None, "head", None),
            P("req", None, "head", None),
            P("req"),
            P("req", None),
            P("req", None),
            P("req", None),
            P("req"),
        ),
        out_specs=P("req", "head"),
        check_vma=False,
    )
```

```python
import jax
import jax.numpy as jnp
from jax import lax
from jax.sharding import PartitionSpec as P

AEXP = 8
CAP = 12


eps = 1e-06
theta = 10000.0


def rotate(vectors, positions):
    half_width = vectors.shape[-1] // 2
    frequency = theta ** (-(jnp.arange(half_width, dtype=jnp.float32) * 2.0) / vectors.shape[-1])
    angles = positions.astype(jnp.float32)[..., None] * frequency
    cosine = jnp.cos(angles)
    sine_part = jnp.sin(angles)
    first_half = vectors[..., :half_width]
    second = vectors[..., half_width:]
    return jnp.concatenate(
        [first_half * cosine - second * sine_part, second * cosine + first_half * sine_part],
        axis=-1,
    )


def body(
    tokens,
    norm_gain,
    key_value_weight,
    query_weight,
    output_weight,
    cache_keys,
    cache_values,
    cache_length,
    page_table,
    expert_choice,
    expert_gate,
    live_mask,
):
    groups = lax.axis_size("req")
    group_index = lax.axis_index("req")
    row_count = tokens.shape[0]
    model_width = tokens.shape[1]
    choices_each = expert_choice.shape[1]
    heads_here = key_value_weight.shape[1]
    head_dim = key_value_weight.shape[3]
    pairs_here = query_weight.shape[0]
    pages_here = cache_keys.shape[0]
    page_len = cache_keys.shape[1]
    max_pages = page_table.shape[1]
    experts = AEXP
    capacity = CAP
    as_float = tokens.astype(jnp.float32)
    normed = (
        as_float
        * lax.rsqrt(jnp.mean(as_float * as_float, axis=-1, keepdims=True) + eps)
        * norm_gain
    ).astype(jnp.bfloat16)
    flat_expert = expert_choice.reshape(-1)
    onehot = (flat_expert[:, None] == jnp.arange(experts)[None, :]).astype(jnp.int32)
    before = jnp.cumsum(onehot, axis=0) - onehot
    slot_index = jnp.sum(before * onehot, axis=1)
    target = flat_expert * capacity + slot_index
    select = target[None, :] == jnp.arange(experts * capacity)[:, None]
    select_rows = select.astype(jnp.bfloat16)
    lanes = 128
    blocks = model_width // lanes
    repeated = jnp.repeat(normed, choices_each, axis=0).reshape(-1, blocks, lanes)
    sendbuf = jnp.einsum(
        "mr,rab->mab", select_rows, repeated, preferred_element_type=jnp.float32
    ).astype(jnp.bfloat16)
    replicas = groups // experts
    sendbuf = jnp.broadcast_to(
        sendbuf.reshape(experts, 1, capacity, blocks, lanes),
        (experts, replicas, capacity, blocks, lanes),
    )
    sendbuf = sendbuf.reshape(groups, capacity * blocks, lanes)
    tokens_far = lax.all_to_all(sendbuf, "req", split_axis=0, concat_axis=0, tiled=True)
    queries_far = jnp.einsum(
        "snab,pabh->spnh",
        tokens_far.reshape(groups, capacity, blocks, lanes),
        query_weight.reshape(pairs_here, blocks, lanes, head_dim),
        preferred_element_type=jnp.float32,
    ).astype(jnp.bfloat16)
    key_value = jnp.einsum(
        "rf,fhkd->rhkd", normed, key_value_weight, preferred_element_type=jnp.float32
    )
    key_new = rotate(key_value[:, :, 0], cache_length[:, None]).astype(jnp.bfloat16)
    value_new = key_value[:, :, 1].astype(jnp.bfloat16)
    local_ids = page_table - group_index * pages_here
    page_used = jnp.arange(max_pages)[None, :] * page_len < cache_length[:, None]
    page_match = page_used[:, :, None] & (
        local_ids[:, :, None] == jnp.arange(pages_here)[None, None, :]
    )
    owned_pages = jnp.any(page_match, axis=1)
    page_taken = jnp.any(owned_pages, axis=0)
    page_owner = jnp.sum(
        owned_pages.astype(jnp.int32) * jnp.arange(row_count, dtype=jnp.int32)[:, None], axis=0
    )
    page_start = jnp.sum(
        page_match.astype(jnp.int32)
        * (jnp.arange(max_pages, dtype=jnp.int32) * page_len)[None, :, None],
        axis=(0, 1),
    )
    page_limit = cache_length[page_owner]
    in_range = page_taken[:, None] & (
        page_start[:, None] + jnp.arange(page_len)[None, :] < page_limit[:, None]
    )
    queries = lax.all_to_all(queries_far, "req", split_axis=0, concat_axis=0, tiled=True)
    queries = (
        queries.reshape(experts, heads_here, capacity, head_dim)
        .transpose(0, 2, 1, 3)
        .reshape(experts * capacity, heads_here, head_dim)
    )
    raw_query = queries[target].reshape(row_count, choices_each, heads_here, head_dim)
    query_rot = rotate(raw_query.astype(jnp.float32), cache_length[:, None, None]).astype(
        jnp.bfloat16
    )
    score_scale = 1.0 / head_dim**0.5
    page_queries = query_rot[page_owner]
    head_eye = jnp.eye(heads_here, dtype=jnp.bfloat16)
    spread_queries = page_queries[:, :, :, None, :] * head_eye[None, None, :, :, None]
    scores = (
        jnp.einsum(
            "pkjhd,pthd->pkjt", spread_queries, cache_keys, preferred_element_type=jnp.float32
        )
        * score_scale
    )
    scores = jnp.where(in_range[:, None, None, :], scores, -jnp.inf)
    fresh_score = (
        jnp.einsum("rkhd,rhd->rkh", query_rot, key_new, preferred_element_type=jnp.float32)
        * score_scale
    )
    page_top = jnp.max(scores, axis=3)
    owned_top = jnp.max(jnp.where(owned_pages[:, :, None, None], page_top[None], -jnp.inf), axis=1)
    row_top = jnp.maximum(owned_top, fresh_score)
    weights = jnp.exp(scores - row_top[page_owner][..., None])
    fresh_weight = jnp.exp(fresh_score - row_top)
    owned_float = owned_pages.astype(jnp.float32)
    denominator = (
        jnp.einsum(
            "rp,pkh->rkh", owned_float, jnp.sum(weights, axis=3), precision=lax.Precision.HIGHEST
        )
        + fresh_weight
    )
    weights_rounded = weights.astype(jnp.bfloat16)
    fresh_rounded = lax.optimization_barrier(fresh_weight.astype(jnp.bfloat16)).astype(jnp.float32)
    page_context = jnp.einsum(
        "pkjt,pthd->pkjhd", weights_rounded, cache_values, preferred_element_type=jnp.float32
    )
    page_context = jnp.sum(page_context * head_eye.astype(jnp.float32)[None, None, :, :, None], axis=3)
    accumulated = jnp.einsum(
        "rp,pkhd->rkhd", owned_float, page_context, precision=lax.Precision.HIGHEST
    )
    accumulated = accumulated + fresh_rounded[..., None] * value_new.astype(jnp.float32)[:, None]
    context = (accumulated / denominator[..., None]).astype(jnp.bfloat16)
    context_flat = context.reshape(row_count * choices_each, heads_here * head_dim)
    context_buf = jnp.dot(select_rows, context_flat, preferred_element_type=jnp.float32).astype(
        jnp.bfloat16
    )
    context_buf = context_buf.reshape(experts, capacity, heads_here, head_dim).transpose(0, 2, 1, 3)
    context_buf = context_buf.reshape(groups, pairs_here, capacity, head_dim)
    head_count = lax.axis_size("head")
    width_here = model_width // head_count
    wblocks = width_here // lanes
    partial_far = jnp.einsum(
        "spnh,phcab->scnab",
        lax.all_to_all(context_buf, "req", split_axis=0, concat_axis=0, tiled=True),
        output_weight.reshape(pairs_here, head_dim, head_count, wblocks, lanes),
        preferred_element_type=jnp.float32,
    )
    gate_flat = expert_gate.reshape(-1)
    spread = (
        jnp.where(select, gate_flat[None, :], jnp.float32(0.0))
        .reshape(experts * capacity, row_count, choices_each)
        .sum(axis=2)
        .T
    )
    alive_rows = live_mask.astype(jnp.float32)[:, None]
    returned = lax.all_to_all(
        partial_far.reshape(groups * head_count, capacity * wblocks, lanes),
        ("req", "head"),
        split_axis=0,
        concat_axis=0,
        tiled=True,
    )
    summed = returned.reshape(experts, replicas * head_count, capacity * wblocks, lanes).sum(axis=1)
    result = jnp.einsum(
        "rm,mab->rab",
        spread,
        summed.reshape(experts * capacity, wblocks, lanes),
        precision=lax.Precision.HIGHEST,
    ).reshape(row_count, width_here)
    return (result * alive_rows).astype(jnp.bfloat16)


def solution(mesh):
    return jax.shard_map(
        body,
        mesh=mesh,
        in_specs=(
            P("req", None),
            P(),
            P(None, "head", None, None),
            P("req", None, "head"),
            P("req", "head", None),
            P("req", None, "head", None),
            P("req", None, "head", None),
            P("req"),
            P("req", None),
            P("req", None),
            P("req", None),
            P("req"),
        ),
        out_specs=P("req", "head"),
        check_vma=False,
    )
```

```python
import jax
import jax.numpy as jnp
from jax import lax
from jax.sharding import PartitionSpec as P

AEXP = 8
CAP = 12


eps = 1e-06
theta = 10000.0


def rotate(vectors, positions):
    half_width = vectors.shape[-1] // 2
    frequency = theta ** (-(jnp.arange(half_width, dtype=jnp.float32) * 2.0) / vectors.shape[-1])
    angles = positions.astype(jnp.float32)[..., None] * frequency
    cosine = jnp.cos(angles)
    sine_part = jnp.sin(angles)
    first_half = vectors[..., :half_width]
    second = vectors[..., half_width:]
    return jnp.concatenate(
        [first_half * cosine - second * sine_part, second * cosine + first_half * sine_part],
        axis=-1,
    )


def body(
    tokens,
    norm_gain,
    key_value_weight,
    query_weight,
    output_weight,
    cache_keys,
    cache_values,
    cache_length,
    page_table,
    expert_choice,
    expert_gate,
    live_mask,
):
    groups = lax.axis_size("req")
    group_index = lax.axis_index("req")
    row_count = tokens.shape[0]
    model_width = tokens.shape[1]
    choices_each = expert_choice.shape[1]
    heads_here = key_value_weight.shape[1]
    head_dim = key_value_weight.shape[3]
    pairs_here = query_weight.shape[0]
    pages_here = cache_keys.shape[0]
    page_len = cache_keys.shape[1]
    max_pages = page_table.shape[1]
    experts = AEXP
    capacity = CAP
    as_float = tokens.astype(jnp.float32)
    normed = (
        as_float
        * lax.rsqrt(jnp.mean(as_float * as_float, axis=-1, keepdims=True) + eps)
        * norm_gain
    ).astype(jnp.bfloat16)
    flat_expert = expert_choice.reshape(-1)
    onehot = (flat_expert[:, None] == jnp.arange(experts)[None, :]).astype(jnp.int32)
    before = jnp.cumsum(onehot, axis=0) - onehot
    slot_index = jnp.sum(before * onehot, axis=1)
    target = flat_expert * capacity + slot_index
    select = target[None, :] == jnp.arange(experts * capacity)[:, None]
    select_rows = select.astype(jnp.bfloat16)
    lanes = 128
    blocks = model_width // lanes
    repeated = jnp.repeat(normed, choices_each, axis=0).reshape(-1, blocks, lanes)
    sendbuf = jnp.einsum(
        "mr,rab->mab", select_rows, repeated, preferred_element_type=jnp.float32
    ).astype(jnp.bfloat16)
    replicas = groups // experts
    sendbuf = jnp.broadcast_to(
        sendbuf.reshape(experts, 1, capacity, blocks, lanes),
        (experts, replicas, capacity, blocks, lanes),
    )
    sendbuf = sendbuf.reshape(groups, capacity * blocks, lanes)
    tokens_far = lax.all_to_all(sendbuf, "req", split_axis=0, concat_axis=0, tiled=True)
    queries_far = jnp.einsum(
        "snab,pabh->spnh",
        tokens_far.reshape(groups, capacity, blocks, lanes),
        query_weight.reshape(pairs_here, blocks, lanes, head_dim),
        preferred_element_type=jnp.float32,
    ).astype(jnp.bfloat16)
    key_value = jnp.einsum(
        "rf,fhkd->rhkd", normed, key_value_weight, preferred_element_type=jnp.float32
    )
    key_new = rotate(key_value[:, :, 0], cache_length[:, None]).astype(jnp.bfloat16)
    value_new = key_value[:, :, 1].astype(jnp.bfloat16)
    local_ids = page_table - group_index * pages_here
    page_used = jnp.arange(max_pages)[None, :] * page_len < cache_length[:, None]
    page_match = page_used[:, :, None] & (
        local_ids[:, :, None] == jnp.arange(pages_here)[None, None, :]
    )
    owned_pages = jnp.any(page_match, axis=1)
    page_taken = jnp.any(owned_pages, axis=0)
    page_owner = jnp.sum(
        owned_pages.astype(jnp.int32) * jnp.arange(row_count, dtype=jnp.int32)[:, None], axis=0
    )
    page_start = jnp.sum(
        page_match.astype(jnp.int32)
        * (jnp.arange(max_pages, dtype=jnp.int32) * page_len)[None, :, None],
        axis=(0, 1),
    )
    page_limit = cache_length[page_owner]
    in_range = page_taken[:, None] & (
        page_start[:, None] + jnp.arange(page_len)[None, :] < page_limit[:, None]
    )
    queries = lax.all_to_all(queries_far, "req", split_axis=0, concat_axis=0, tiled=True)
    queries = (
        queries.reshape(experts, heads_here, capacity, head_dim)
        .transpose(0, 2, 1, 3)
        .reshape(experts * capacity, heads_here, head_dim)
    )
    raw_query = queries[target].reshape(row_count, choices_each, heads_here, head_dim)
    query_rot = rotate(raw_query.astype(jnp.float32), cache_length[:, None, None]).astype(
        jnp.bfloat16
    )
    score_scale = 1.0 / head_dim**0.5
    page_queries = query_rot[page_owner]
    head_eye = jnp.eye(heads_here, dtype=jnp.bfloat16)
    spread_queries = page_queries[:, :, :, None, :] * head_eye[None, None, :, :, None]
    scores = (
        jnp.einsum(
            "pkjhd,pthd->pkjt", spread_queries, cache_keys, preferred_element_type=jnp.float32
        )
        * score_scale
    )
    scores = jnp.where(in_range[:, None, None, :], scores, -jnp.inf)
    fresh_score = (
        jnp.einsum("rkhd,rhd->rkh", query_rot, key_new, preferred_element_type=jnp.float32)
        * score_scale
    )
    page_top = jnp.max(scores, axis=3)
    owned_top = jnp.max(jnp.where(owned_pages[:, :, None, None], page_top[None], -jnp.inf), axis=1)
    row_top = jnp.maximum(owned_top, fresh_score)
    weights = jnp.exp(scores - row_top[page_owner][..., None])
    fresh_weight = jnp.exp(fresh_score - row_top)
    owned_float = owned_pages.astype(jnp.float32)
    denominator = (
        jnp.einsum(
            "rp,pkh->rkh", owned_float, jnp.sum(weights, axis=3), precision=lax.Precision.HIGHEST
        )
        + fresh_weight
    )
    weights_rounded = weights.astype(jnp.bfloat16)
    fresh_rounded = lax.optimization_barrier(fresh_weight.astype(jnp.bfloat16)).astype(jnp.float32)
    page_context = jnp.einsum(
        "pkjt,pthd->pkjhd", weights_rounded, cache_values, preferred_element_type=jnp.float32
    )
    page_context = jnp.sum(page_context * head_eye.astype(jnp.float32)[None, None, :, :, None], axis=3)
    accumulated = jnp.einsum(
        "rp,pkhd->rkhd", owned_float, page_context, precision=lax.Precision.HIGHEST
    )
    accumulated = accumulated + fresh_rounded[..., None] * value_new.astype(jnp.float32)[:, None]
    context = (accumulated / denominator[..., None]).astype(jnp.bfloat16)
    context_flat = context.reshape(row_count * choices_each, heads_here * head_dim)
    context_buf = jnp.dot(select_rows, context_flat, preferred_element_type=jnp.float32).astype(
        jnp.bfloat16
    )
    context_buf = context_buf.reshape(experts, capacity, heads_here, head_dim).transpose(0, 2, 1, 3)
    context_buf = context_buf.reshape(groups, pairs_here, capacity, head_dim)
    head_count = lax.axis_size("head")
    width_here = model_width // head_count
    wblocks = width_here // lanes
    partial_far = jnp.einsum(
        "spnh,phd->snd",
        lax.all_to_all(context_buf, "req", split_axis=0, concat_axis=0, tiled=True),
        output_weight,
        preferred_element_type=jnp.float32,
    )
    partial_far = partial_far.reshape(groups, capacity, head_count, wblocks, lanes).transpose(
        0, 2, 1, 3, 4
    )
    gate_flat = expert_gate.reshape(-1)
    spread = (
        jnp.where(select, gate_flat[None, :], jnp.float32(0.0))
        .reshape(experts * capacity, row_count, choices_each)
        .sum(axis=2)
        .T
    )
    alive_rows = live_mask.astype(jnp.float32)[:, None]
    returned = lax.all_to_all(
        partial_far.reshape(groups * head_count, capacity * wblocks, lanes),
        ("req", "head"),
        split_axis=0,
        concat_axis=0,
        tiled=True,
    )
    summed = returned.reshape(experts, replicas * head_count, capacity * wblocks, lanes).sum(axis=1)
    result = jnp.einsum(
        "rm,mab->rab",
        spread,
        summed.reshape(experts * capacity, wblocks, lanes),
        precision=lax.Precision.HIGHEST,
    ).reshape(row_count, width_here)
    return (result * alive_rows).astype(jnp.bfloat16)


def solution(mesh):
    return jax.shard_map(
        body,
        mesh=mesh,
        in_specs=(
            P("req", None),
            P(),
            P(None, "head", None, None),
            P("req", None, "head"),
            P("req", "head", None),
            P("req", None, "head", None),
            P("req", None, "head", None),
            P("req"),
            P("req", None),
            P("req", None),
            P("req", None),
            P("req"),
        ),
        out_specs=P("req", "head"),
        check_vma=False,
    )
```

```python
import jax
import jax.numpy as jnp
from jax import lax
from jax.sharding import PartitionSpec as P

AEXP = 8
CAP = 12


eps = 1e-06
theta = 10000.0


def rotate(vectors, positions):
    half_width = vectors.shape[-1] // 2
    frequency = theta ** (-(jnp.arange(half_width, dtype=jnp.float32) * 2.0) / vectors.shape[-1])
    angles = positions.astype(jnp.float32)[..., None] * frequency
    cosine = jnp.cos(angles)
    sine_part = jnp.sin(angles)
    first_half = vectors[..., :half_width]
    second = vectors[..., half_width:]
    return jnp.concatenate(
        [first_half * cosine - second * sine_part, second * cosine + first_half * sine_part],
        axis=-1,
    )


def body(
    tokens,
    norm_gain,
    key_value_weight,
    query_weight,
    output_weight,
    cache_keys,
    cache_values,
    cache_length,
    page_table,
    expert_choice,
    expert_gate,
    live_mask,
):
    groups = lax.axis_size("req")
    group_index = lax.axis_index("req")
    row_count = tokens.shape[0]
    model_width = tokens.shape[1]
    choices_each = expert_choice.shape[1]
    heads_here = key_value_weight.shape[1]
    head_dim = key_value_weight.shape[3]
    pairs_here = query_weight.shape[0]
    pages_here = cache_keys.shape[0]
    page_len = cache_keys.shape[1]
    max_pages = page_table.shape[1]
    experts = AEXP
    capacity = CAP
    as_float = tokens.astype(jnp.float32)
    normed = (
        as_float
        * lax.rsqrt(jnp.mean(as_float * as_float, axis=-1, keepdims=True) + eps)
        * norm_gain
    ).astype(jnp.bfloat16)
    choice_major = jnp.concatenate([expert_choice[:, k] for k in range(choices_each)])
    onehot = (choice_major[:, None] == jnp.arange(experts)[None, :]).astype(jnp.int32)
    before = jnp.cumsum(onehot, axis=0) - onehot
    slot_index = jnp.sum(before * onehot, axis=1)
    target = (choice_major * capacity + slot_index).reshape(choices_each, row_count).T.reshape(-1)
    select = target[None, :] == jnp.arange(experts * capacity)[:, None]
    select_rows = select.astype(jnp.bfloat16)
    lanes = 128
    blocks = model_width // lanes
    slot_used = jnp.any(select, axis=1)
    slot_row = jnp.sum(
        select.astype(jnp.int32) * jnp.arange(row_count * choices_each, dtype=jnp.int32)[None, :],
        axis=1,
    ) // choices_each
    sendbuf = jnp.where(
        slot_used[:, None, None],
        normed.reshape(row_count, blocks, lanes)[slot_row],
        jnp.zeros((), jnp.bfloat16),
    )
    replicas = groups // experts
    sendbuf = jnp.broadcast_to(
        sendbuf.reshape(experts, 1, capacity, blocks, lanes),
        (experts, replicas, capacity, blocks, lanes),
    )
    sendbuf = sendbuf.reshape(groups, capacity * blocks, lanes)
    tokens_far = lax.all_to_all(sendbuf, "req", split_axis=0, concat_axis=0, tiled=True)
    queries_far = jnp.einsum(
        "snab,pabh->spnh",
        tokens_far.reshape(groups, capacity, blocks, lanes),
        query_weight.reshape(pairs_here, blocks, lanes, head_dim),
        preferred_element_type=jnp.float32,
    ).astype(jnp.bfloat16)
    key_value = jnp.einsum(
        "rf,fhkd->rhkd", normed, key_value_weight, preferred_element_type=jnp.float32
    )
    key_new = rotate(key_value[:, :, 0], cache_length[:, None]).astype(jnp.bfloat16)
    value_new = key_value[:, :, 1].astype(jnp.bfloat16)
    local_ids = page_table - group_index * pages_here
    page_used = jnp.arange(max_pages)[None, :] * page_len < cache_length[:, None]
    page_match = page_used[:, :, None] & (
        local_ids[:, :, None] == jnp.arange(pages_here)[None, None, :]
    )
    owned_pages = jnp.any(page_match, axis=1)
    page_taken = jnp.any(owned_pages, axis=0)
    page_owner = jnp.sum(
        owned_pages.astype(jnp.int32) * jnp.arange(row_count, dtype=jnp.int32)[:, None], axis=0
    )
    page_start = jnp.sum(
        page_match.astype(jnp.int32)
        * (jnp.arange(max_pages, dtype=jnp.int32) * page_len)[None, :, None],
        axis=(0, 1),
    )
    page_limit = cache_length[page_owner]
    in_range = page_taken[:, None] & (
        page_start[:, None] + jnp.arange(page_len)[None, :] < page_limit[:, None]
    )
    queries = lax.all_to_all(queries_far, "req", split_axis=0, concat_axis=0, tiled=True)
    queries = (
        queries.reshape(experts, heads_here, capacity, head_dim)
        .transpose(0, 2, 1, 3)
        .reshape(experts * capacity, heads_here, head_dim)
    )
    pair_target = target.reshape(row_count, choices_each)
    raw_query = queries[pair_target]
    query_rot = rotate(raw_query.astype(jnp.float32), cache_length[:, None, None]).astype(
        jnp.bfloat16
    )
    page_raw = queries[pair_target[page_owner]]
    page_queries = rotate(page_raw.astype(jnp.float32), page_limit[:, None, None]).astype(
        jnp.bfloat16
    )
    score_scale = 1.0 / head_dim**0.5
    head_eye = jnp.eye(heads_here, dtype=jnp.bfloat16)
    spread_queries = page_queries[:, :, :, None, :] * head_eye[None, None, :, :, None]
    scores = (
        jnp.einsum(
            "pkjhd,pthd->pkjt", spread_queries, cache_keys, preferred_element_type=jnp.float32
        )
        * score_scale
    )
    scores = jnp.where(in_range[:, None, None, :], scores, -jnp.inf)
    fresh_score = (
        jnp.einsum("rkhd,rhd->rkh", query_rot, key_new, preferred_element_type=jnp.float32)
        * score_scale
    )
    page_top = jnp.max(scores, axis=3)
    owned_top = jnp.max(jnp.where(owned_pages[:, :, None, None], page_top[None], -jnp.inf), axis=1)
    row_top = jnp.maximum(owned_top, fresh_score)
    weights = jnp.exp(scores - row_top[page_owner][..., None])
    fresh_weight = jnp.exp(fresh_score - row_top)
    owned_float = owned_pages.astype(jnp.float32)
    denominator = (
        jnp.einsum(
            "rp,pkh->rkh", owned_float, jnp.sum(weights, axis=3), precision=lax.Precision.HIGHEST
        )
        + fresh_weight
    )
    weights_rounded = weights.astype(jnp.bfloat16)
    fresh_rounded = lax.optimization_barrier(fresh_weight.astype(jnp.bfloat16)).astype(jnp.float32)
    page_context = jnp.einsum(
        "pkjt,pthd->pkjhd", weights_rounded, cache_values, preferred_element_type=jnp.float32
    )
    page_context = jnp.sum(page_context * head_eye.astype(jnp.float32)[None, None, :, :, None], axis=3)
    accumulated = jnp.einsum(
        "rp,pkhd->rkhd", owned_float, page_context, precision=lax.Precision.HIGHEST
    )
    accumulated = accumulated + fresh_rounded[..., None] * value_new.astype(jnp.float32)[:, None]
    context = (accumulated / denominator[..., None]).astype(jnp.bfloat16)
    context_flat = context.reshape(row_count * choices_each, heads_here * head_dim)
    context_buf = jnp.dot(select_rows, context_flat, preferred_element_type=jnp.float32).astype(
        jnp.bfloat16
    )
    context_buf = context_buf.reshape(experts, capacity, heads_here, head_dim).transpose(0, 2, 1, 3)
    context_buf = context_buf.reshape(groups, pairs_here, capacity, head_dim)
    head_count = lax.axis_size("head")
    width_here = model_width // head_count
    wblocks = width_here // lanes
    partial_far = jnp.einsum(
        "spnh,phd->snd",
        lax.all_to_all(context_buf, "req", split_axis=0, concat_axis=0, tiled=True),
        output_weight,
        preferred_element_type=jnp.float32,
    )
    partial_far = partial_far.reshape(groups, capacity, head_count, wblocks, lanes).transpose(
        0, 2, 1, 3, 4
    )
    gate_flat = expert_gate.reshape(-1)
    spread = (
        jnp.where(select, gate_flat[None, :], jnp.float32(0.0))
        .reshape(experts * capacity, row_count, choices_each)
        .sum(axis=2)
        .T
    )
    alive_rows = live_mask.astype(jnp.float32)[:, None]
    returned = lax.all_to_all(
        partial_far.reshape(groups * head_count, capacity * wblocks, lanes),
        ("req", "head"),
        split_axis=0,
        concat_axis=0,
        tiled=True,
    )
    summed = returned.reshape(experts, replicas * head_count, capacity * wblocks, lanes).sum(axis=1)
    result = jnp.einsum(
        "rm,mab->rab",
        spread,
        summed.reshape(experts * capacity, wblocks, lanes),
        precision=lax.Precision.HIGHEST,
    ).reshape(row_count, width_here)
    return (result * alive_rows).astype(jnp.bfloat16)


def solution(mesh):
    return jax.shard_map(
        body,
        mesh=mesh,
        in_specs=(
            P("req", None),
            P(),
            P(None, "head", None, None),
            P("req", None, "head"),
            P("req", "head", None),
            P("req", None, "head", None),
            P("req", None, "head", None),
            P("req"),
            P("req", None),
            P("req", None),
            P("req", None),
            P("req"),
        ),
        out_specs=P("req", "head"),
        check_vma=False,
    )
```

```python
import jax
import jax.numpy as jnp
from jax import lax
from jax.sharding import PartitionSpec as P

AEXP = 8
CAP = 12


eps = 1e-06
theta = 10000.0


def rotate(vectors, positions):
    half_width = vectors.shape[-1] // 2
    frequency = theta ** (-(jnp.arange(half_width, dtype=jnp.float32) * 2.0) / vectors.shape[-1])
    angles = positions.astype(jnp.float32)[..., None] * frequency
    cosine = jnp.cos(angles)
    sine_part = jnp.sin(angles)
    first_half = vectors[..., :half_width]
    second = vectors[..., half_width:]
    return jnp.concatenate(
        [first_half * cosine - second * sine_part, second * cosine + first_half * sine_part],
        axis=-1,
    )


def body(
    tokens,
    norm_gain,
    key_value_weight,
    query_weight,
    output_weight,
    cache_keys,
    cache_values,
    cache_length,
    page_table,
    expert_choice,
    expert_gate,
    live_mask,
):
    groups = lax.axis_size("req")
    group_index = lax.axis_index("req")
    row_count = tokens.shape[0]
    model_width = tokens.shape[1]
    choices_each = expert_choice.shape[1]
    heads_here = key_value_weight.shape[1]
    head_dim = key_value_weight.shape[3]
    pairs_here = query_weight.shape[0]
    pages_here = cache_keys.shape[0]
    page_len = cache_keys.shape[1]
    max_pages = page_table.shape[1]
    experts = AEXP
    capacity = CAP
    as_float = tokens.astype(jnp.float32)
    normed = (
        as_float
        * lax.rsqrt(jnp.mean(as_float * as_float, axis=-1, keepdims=True) + eps)
        * norm_gain
    ).astype(jnp.bfloat16)
    flat_expert = expert_choice.reshape(-1)
    onehot = (flat_expert[:, None] == jnp.arange(experts)[None, :]).astype(jnp.int32)
    before = jnp.cumsum(onehot, axis=0) - onehot
    slot_index = jnp.sum(before * onehot, axis=1)
    target = flat_expert * capacity + slot_index
    select = target[None, :] == jnp.arange(experts * capacity)[:, None]
    select_rows = select.astype(jnp.bfloat16)
    lanes = 128
    blocks = model_width // lanes
    repeated = jnp.repeat(normed, choices_each, axis=0).reshape(-1, blocks, lanes)
    sendbuf = jnp.einsum(
        "mr,rab->mab", select_rows, repeated, preferred_element_type=jnp.float32
    ).astype(jnp.bfloat16)
    replicas = groups // experts
    sendbuf = jnp.broadcast_to(
        sendbuf.reshape(experts, 1, capacity, blocks, lanes),
        (experts, replicas, capacity, blocks, lanes),
    )
    sendbuf = sendbuf.reshape(groups, capacity * blocks, lanes)
    tokens_far = lax.all_to_all(sendbuf, "req", split_axis=0, concat_axis=0, tiled=True)
    queries_far = jnp.einsum(
        "snab,pabh->spnh",
        tokens_far.reshape(groups, capacity, blocks, lanes),
        query_weight.reshape(pairs_here, blocks, lanes, head_dim),
        preferred_element_type=jnp.float32,
    ).astype(jnp.bfloat16)
    key_value = jnp.einsum(
        "rf,fhkd->rhkd", normed, key_value_weight, preferred_element_type=jnp.float32
    )
    key_new = rotate(key_value[:, :, 0], cache_length[:, None]).astype(jnp.bfloat16)
    value_new = key_value[:, :, 1].astype(jnp.bfloat16)
    local_ids = page_table - group_index * pages_here
    page_used = jnp.arange(max_pages)[None, :] * page_len < cache_length[:, None]
    page_match = page_used[:, :, None] & (
        local_ids[:, :, None] == jnp.arange(pages_here)[None, None, :]
    )
    owned_pages = jnp.any(page_match, axis=1)
    page_taken = jnp.any(owned_pages, axis=0)
    page_owner = jnp.sum(
        owned_pages.astype(jnp.int32) * jnp.arange(row_count, dtype=jnp.int32)[:, None], axis=0
    )
    page_start = jnp.sum(
        page_match.astype(jnp.int32)
        * (jnp.arange(max_pages, dtype=jnp.int32) * page_len)[None, :, None],
        axis=(0, 1),
    )
    page_limit = cache_length[page_owner]
    in_range = page_taken[:, None] & (
        page_start[:, None] + jnp.arange(page_len)[None, :] < page_limit[:, None]
    )
    queries = lax.all_to_all(queries_far, "req", split_axis=0, concat_axis=0, tiled=True)
    queries = (
        queries.reshape(experts, heads_here, capacity, head_dim)
        .transpose(0, 2, 1, 3)
        .reshape(experts * capacity, heads_here, head_dim)
    )
    raw_query = queries[target].reshape(row_count, choices_each, heads_here, head_dim)
    query_rot = rotate(raw_query.astype(jnp.float32), cache_length[:, None, None]).astype(
        jnp.bfloat16
    )
    score_scale = 1.0 / head_dim**0.5
    page_queries = query_rot[page_owner]
    head_eye = jnp.eye(heads_here, dtype=jnp.bfloat16)
    spread_queries = page_queries[:, :, :, None, :] * head_eye[None, None, :, :, None]
    scores = (
        jnp.einsum(
            "pkjhd,pthd->pkjt", spread_queries, cache_keys, preferred_element_type=jnp.float32
        )
        * score_scale
    )
    scores = jnp.where(in_range[:, None, None, :], scores, -jnp.inf)
    fresh_score = (
        jnp.einsum("rkhd,rhd->rkh", query_rot, key_new, preferred_element_type=jnp.float32)
        * score_scale
    )
    page_top = jnp.max(scores, axis=3)
    owned_top = jnp.max(jnp.where(owned_pages[:, :, None, None], page_top[None], -jnp.inf), axis=1)
    row_top = jnp.maximum(owned_top, fresh_score)
    weights = jnp.exp(scores - row_top[page_owner][..., None])
    fresh_weight = jnp.exp(fresh_score - row_top)
    owned_float = owned_pages.astype(jnp.float32)
    denominator = (
        jnp.einsum(
            "rp,pkh->rkh", owned_float, jnp.sum(weights, axis=3), precision=lax.Precision.HIGHEST
        )
        + fresh_weight
    )
    weights_rounded = weights.astype(jnp.bfloat16)
    fresh_rounded = lax.optimization_barrier(fresh_weight.astype(jnp.bfloat16)).astype(jnp.float32)
    page_context = jnp.einsum(
        "pkjt,pthd->pkjhd", weights_rounded, cache_values, preferred_element_type=jnp.float32
    )
    page_context = jnp.sum(page_context * head_eye.astype(jnp.float32)[None, None, :, :, None], axis=3)
    accumulated = jnp.einsum(
        "rp,pkhd->rkhd", owned_float, page_context, precision=lax.Precision.HIGHEST
    )
    accumulated = accumulated + fresh_rounded[..., None] * value_new.astype(jnp.float32)[:, None]
    context = (accumulated / denominator[..., None]).astype(jnp.bfloat16)
    context_flat = context.reshape(row_count * choices_each, heads_here * head_dim)
    context_buf = jnp.dot(select_rows, context_flat, preferred_element_type=jnp.float32).astype(
        jnp.bfloat16
    )
    context_buf = context_buf.reshape(experts, capacity, heads_here, head_dim).transpose(0, 2, 1, 3)
    context_buf = context_buf.reshape(groups, pairs_here, capacity, head_dim)
    head_count = lax.axis_size("head")
    width_here = model_width // head_count
    wblocks = width_here // lanes
    partial_far = jnp.einsum(
        "spnh,phd->snd",
        lax.all_to_all(context_buf, "req", split_axis=0, concat_axis=0, tiled=True),
        output_weight,
        preferred_element_type=jnp.float32,
    )
    head_index = lax.axis_index("head")
    held = partial_far.reshape(groups, capacity, head_count, width_here)
    bit = 1
    while bit < head_count:
        pair = held.reshape(groups, capacity, held.shape[2] // 2, 2, width_here)
        upper = (head_index // bit) % 2 == 1
        keep = jnp.where(upper, pair[:, :, :, 1], pair[:, :, :, 0])
        give = jnp.where(upper, pair[:, :, :, 0], pair[:, :, :, 1])
        got = lax.ppermute(give, "head", [(c, c ^ bit) for c in range(head_count)])
        held = keep + got
        bit *= 2
    gate_flat = expert_gate.reshape(-1)
    spread = (
        jnp.where(select, gate_flat[None, :], jnp.float32(0.0))
        .reshape(experts * capacity, row_count, choices_each)
        .sum(axis=2)
        .T
    )
    alive_rows = live_mask.astype(jnp.float32)[:, None]
    returned = lax.all_to_all(
        held.reshape(groups, capacity * wblocks, lanes),
        "req",
        split_axis=0,
        concat_axis=0,
        tiled=True,
    )
    summed = returned.reshape(experts, replicas, capacity * wblocks, lanes).sum(axis=1)
    result = jnp.einsum(
        "rm,mab->rab",
        spread,
        summed.reshape(experts * capacity, wblocks, lanes),
        precision=lax.Precision.HIGHEST,
    ).reshape(row_count, width_here)
    return (result * alive_rows).astype(jnp.bfloat16)


def solution(mesh):
    return jax.shard_map(
        body,
        mesh=mesh,
        in_specs=(
            P("req", None),
            P(),
            P(None, "head", None, None),
            P("req", None, "head"),
            P("req", "head", None),
            P("req", None, "head", None),
            P("req", None, "head", None),
            P("req"),
            P("req", None),
            P("req", None),
            P("req", None),
            P("req"),
        ),
        out_specs=P("req", "head"),
        check_vma=False,
    )
```

```python
import jax
import jax.numpy as jnp
from jax import lax
from jax.sharding import PartitionSpec as P

AEXP = 8
CAP = 12


eps = 1e-06
theta = 10000.0


def rotate(vectors, positions):
    half_width = vectors.shape[-1] // 2
    frequency = theta ** (-(jnp.arange(half_width, dtype=jnp.float32) * 2.0) / vectors.shape[-1])
    angles = positions.astype(jnp.float32)[..., None] * frequency
    cosine = jnp.cos(angles)
    sine_part = jnp.sin(angles)
    first_half = vectors[..., :half_width]
    second = vectors[..., half_width:]
    return jnp.concatenate(
        [first_half * cosine - second * sine_part, second * cosine + first_half * sine_part],
        axis=-1,
    )


def body(
    tokens,
    norm_gain,
    key_value_weight,
    query_weight,
    output_weight,
    cache_keys,
    cache_values,
    cache_length,
    page_table,
    expert_choice,
    expert_gate,
    live_mask,
):
    groups = lax.axis_size("req")
    group_index = lax.axis_index("req")
    row_count = tokens.shape[0]
    model_width = tokens.shape[1]
    choices_each = expert_choice.shape[1]
    heads_here = key_value_weight.shape[1]
    head_dim = key_value_weight.shape[3]
    pairs_here = query_weight.shape[0]
    pages_here = cache_keys.shape[0]
    page_len = cache_keys.shape[1]
    max_pages = page_table.shape[1]
    experts = AEXP
    capacity = CAP
    as_float = tokens.astype(jnp.float32)
    normed = (
        as_float
        * lax.rsqrt(jnp.mean(as_float * as_float, axis=-1, keepdims=True) + eps)
        * norm_gain
    ).astype(jnp.bfloat16)
    flat_expert = expert_choice.reshape(-1)
    onehot = (flat_expert[:, None] == jnp.arange(experts)[None, :]).astype(jnp.int32)
    before = jnp.cumsum(onehot, axis=0) - onehot
    slot_index = jnp.sum(before * onehot, axis=1)
    target = flat_expert * capacity + slot_index
    select = target[None, :] == jnp.arange(experts * capacity)[:, None]
    select_rows = select.astype(jnp.bfloat16)
    lanes = 128
    blocks = model_width // lanes
    repeated = jnp.repeat(normed, choices_each, axis=0).reshape(-1, blocks, lanes)
    sendbuf = jnp.einsum(
        "mr,rab->mab", select_rows, repeated, preferred_element_type=jnp.float32
    ).astype(jnp.bfloat16)
    replicas = groups // experts
    sendbuf = jnp.broadcast_to(
        sendbuf.reshape(experts, 1, capacity, blocks, lanes),
        (experts, replicas, capacity, blocks, lanes),
    )
    sendbuf = sendbuf.reshape(groups, capacity * blocks, lanes)
    tokens_far = lax.all_to_all(sendbuf, "req", split_axis=0, concat_axis=0, tiled=True)
    queries_far = jnp.einsum(
        "snab,pabh->spnh",
        tokens_far.reshape(groups, capacity, blocks, lanes),
        query_weight.reshape(pairs_here, blocks, lanes, head_dim),
        preferred_element_type=jnp.float32,
    ).astype(jnp.bfloat16)
    key_value = jnp.einsum(
        "rf,fhkd->rhkd", normed, key_value_weight, preferred_element_type=jnp.float32
    )
    key_new = rotate(key_value[:, :, 0], cache_length[:, None]).astype(jnp.bfloat16)
    value_new = key_value[:, :, 1].astype(jnp.bfloat16)
    local_ids = page_table - group_index * pages_here
    page_used = jnp.arange(max_pages)[None, :] * page_len < cache_length[:, None]
    page_match = page_used[:, :, None] & (
        local_ids[:, :, None] == jnp.arange(pages_here)[None, None, :]
    )
    owned_pages = jnp.any(page_match, axis=1)
    page_taken = jnp.any(owned_pages, axis=0)
    page_owner = jnp.sum(
        owned_pages.astype(jnp.int32) * jnp.arange(row_count, dtype=jnp.int32)[:, None], axis=0
    )
    page_start = jnp.sum(
        page_match.astype(jnp.int32)
        * (jnp.arange(max_pages, dtype=jnp.int32) * page_len)[None, :, None],
        axis=(0, 1),
    )
    page_limit = cache_length[page_owner]
    in_range = page_taken[:, None] & (
        page_start[:, None] + jnp.arange(page_len)[None, :] < page_limit[:, None]
    )
    queries = lax.all_to_all(queries_far, "req", split_axis=0, concat_axis=0, tiled=True)
    queries = (
        queries.reshape(experts, heads_here, capacity, head_dim)
        .transpose(0, 2, 1, 3)
        .reshape(experts * capacity, heads_here, head_dim)
    )
    page_slots = target.reshape(row_count, choices_each)[page_owner]
    key_page = key_new[page_owner]
    value_page = value_new[page_owner]
    same_owner = (
        page_taken[:, None] & page_taken[None, :] & (page_owner[:, None] == page_owner[None, :])
    )
    leader = jnp.any(local_ids[:, :1] == jnp.arange(pages_here)[None, :], axis=0)
    leader_float = leader.astype(jnp.float32)[:, None, None]
    page_raw = queries[page_slots]
    page_queries = rotate(page_raw.astype(jnp.float32), page_limit[:, None, None]).astype(
        jnp.bfloat16
    )
    score_scale = 1.0 / head_dim**0.5
    head_eye = jnp.eye(heads_here, dtype=jnp.bfloat16)
    spread_queries = page_queries[:, :, :, None, :] * head_eye[None, None, :, :, None]
    scores = (
        jnp.einsum(
            "pkjhd,pthd->pkjt", spread_queries, cache_keys, preferred_element_type=jnp.float32
        )
        * score_scale
    )
    scores = jnp.where(in_range[:, None, None, :], scores, -jnp.inf)
    fresh_score = (
        jnp.einsum("pkhd,phd->pkh", page_queries, key_page, preferred_element_type=jnp.float32)
        * score_scale
    )
    page_top = jnp.max(scores, axis=3)
    owner_top = jnp.max(jnp.where(same_owner[:, :, None, None], page_top[None], -jnp.inf), axis=1)
    row_top = jnp.maximum(owner_top, fresh_score)
    weights = jnp.exp(scores - row_top[..., None])
    fresh_weight = jnp.exp(fresh_score - row_top)
    owned_float = owned_pages.astype(jnp.float32)
    denominator = jnp.einsum(
        "rp,pkh->rkh",
        owned_float,
        jnp.sum(weights, axis=3) + leader_float * fresh_weight,
        precision=lax.Precision.HIGHEST,
    )
    weights_rounded = weights.astype(jnp.bfloat16)
    fresh_rounded = lax.optimization_barrier(fresh_weight.astype(jnp.bfloat16)).astype(jnp.float32)
    page_context = jnp.einsum(
        "pkjt,pthd->pkjhd", weights_rounded, cache_values, preferred_element_type=jnp.float32
    )
    page_context = jnp.sum(page_context * head_eye.astype(jnp.float32)[None, None, :, :, None], axis=3)
    page_context = page_context + (leader_float * fresh_rounded)[..., None] * value_page.astype(
        jnp.float32
    )[:, None]
    accumulated = jnp.einsum(
        "rp,pkhd->rkhd", owned_float, page_context, precision=lax.Precision.HIGHEST
    )
    context = (accumulated / denominator[..., None]).astype(jnp.bfloat16)
    context_flat = context.reshape(row_count * choices_each, heads_here * head_dim)
    context_buf = jnp.dot(select_rows, context_flat, preferred_element_type=jnp.float32).astype(
        jnp.bfloat16
    )
    context_buf = context_buf.reshape(experts, capacity, heads_here, head_dim).transpose(0, 2, 1, 3)
    context_buf = context_buf.reshape(groups, pairs_here, capacity, head_dim)
    head_count = lax.axis_size("head")
    width_here = model_width // head_count
    wblocks = width_here // lanes
    partial_far = jnp.einsum(
        "spnh,phd->snd",
        lax.all_to_all(context_buf, "req", split_axis=0, concat_axis=0, tiled=True),
        output_weight,
        preferred_element_type=jnp.float32,
    )
    partial_far = partial_far.reshape(groups, capacity, head_count, wblocks, lanes).transpose(
        0, 2, 1, 3, 4
    )
    gate_flat = expert_gate.reshape(-1)
    spread = (
        jnp.where(select, gate_flat[None, :], jnp.float32(0.0))
        .reshape(experts * capacity, row_count, choices_each)
        .sum(axis=2)
        .T
    )
    alive_rows = live_mask.astype(jnp.float32)[:, None]
    returned = lax.all_to_all(
        partial_far.reshape(groups * head_count, capacity * wblocks, lanes),
        ("req", "head"),
        split_axis=0,
        concat_axis=0,
        tiled=True,
    )
    summed = returned.reshape(experts, replicas * head_count, capacity * wblocks, lanes).sum(axis=1)
    result = jnp.einsum(
        "rm,mab->rab",
        spread,
        summed.reshape(experts * capacity, wblocks, lanes),
        precision=lax.Precision.HIGHEST,
    ).reshape(row_count, width_here)
    return (result * alive_rows).astype(jnp.bfloat16)


def solution(mesh):
    return jax.shard_map(
        body,
        mesh=mesh,
        in_specs=(
            P("req", None),
            P(),
            P(None, "head", None, None),
            P("req", None, "head"),
            P("req", "head", None),
            P("req", None, "head", None),
            P("req", None, "head", None),
            P("req"),
            P("req", None),
            P("req", None),
            P("req", None),
            P("req"),
        ),
        out_specs=P("req", "head"),
        check_vma=False,
    )
```

```python
import jax
import jax.numpy as jnp
from jax import lax
from jax.sharding import PartitionSpec as P

AEXP = 8
CAP = 12


eps = 1e-06
theta = 10000.0


def rotate(vectors, positions):
    half_width = vectors.shape[-1] // 2
    frequency = theta ** (-(jnp.arange(half_width, dtype=jnp.float32) * 2.0) / vectors.shape[-1])
    angles = positions.astype(jnp.float32)[..., None] * frequency
    cosine = jnp.cos(angles)
    sine_part = jnp.sin(angles)
    first_half = vectors[..., :half_width]
    second = vectors[..., half_width:]
    return jnp.concatenate(
        [first_half * cosine - second * sine_part, second * cosine + first_half * sine_part],
        axis=-1,
    )


def body(
    tokens,
    norm_gain,
    key_value_weight,
    query_weight,
    output_weight,
    cache_keys,
    cache_values,
    cache_length,
    page_table,
    expert_choice,
    expert_gate,
    live_mask,
):
    groups = lax.axis_size("req")
    group_index = lax.axis_index("req")
    row_count = tokens.shape[0]
    model_width = tokens.shape[1]
    choices_each = expert_choice.shape[1]
    heads_here = key_value_weight.shape[1]
    head_dim = key_value_weight.shape[3]
    pairs_here = query_weight.shape[0]
    pages_here = cache_keys.shape[0]
    page_len = cache_keys.shape[1]
    max_pages = page_table.shape[1]
    experts = AEXP
    capacity = CAP
    as_float = tokens.astype(jnp.float32)
    normed = (
        as_float
        * lax.rsqrt(jnp.mean(as_float * as_float, axis=-1, keepdims=True) + eps)
        * norm_gain
    ).astype(jnp.bfloat16)
    flat_expert = expert_choice.reshape(-1)
    onehot = (flat_expert[:, None] == jnp.arange(experts)[None, :]).astype(jnp.int32)
    before = jnp.cumsum(onehot, axis=0) - onehot
    slot_index = jnp.sum(before * onehot, axis=1)
    target = flat_expert * capacity + slot_index
    select = target[None, :] == jnp.arange(experts * capacity)[:, None]
    select_rows = select.astype(jnp.bfloat16)
    lanes = 128
    blocks = model_width // lanes
    repeated = jnp.repeat(normed, choices_each, axis=0).reshape(-1, blocks, lanes)
    sendbuf = jnp.einsum(
        "mr,rab->mab", select_rows, repeated, preferred_element_type=jnp.float32
    ).astype(jnp.bfloat16)
    replicas = groups // experts
    sendbuf = jnp.broadcast_to(
        sendbuf.reshape(experts, 1, capacity, blocks, lanes),
        (experts, replicas, capacity, blocks, lanes),
    )
    sendbuf = sendbuf.reshape(groups, capacity * blocks, lanes)
    tokens_far = lax.all_to_all(sendbuf, "req", split_axis=0, concat_axis=0, tiled=True)
    queries_far = jnp.einsum(
        "snab,pabh->spnh",
        tokens_far.reshape(groups, capacity, blocks, lanes),
        query_weight.reshape(pairs_here, blocks, lanes, head_dim),
        preferred_element_type=jnp.float32,
    ).astype(jnp.bfloat16)
    key_value = jnp.einsum(
        "rf,fhkd->rhkd", normed, key_value_weight, preferred_element_type=jnp.float32
    )
    key_new = rotate(key_value[:, :, 0], cache_length[:, None]).astype(jnp.bfloat16)
    value_new = key_value[:, :, 1].astype(jnp.bfloat16)
    local_ids = page_table - group_index * pages_here
    page_used = jnp.arange(max_pages)[None, :] * page_len < cache_length[:, None]
    page_match = page_used[:, :, None] & (
        local_ids[:, :, None] == jnp.arange(pages_here)[None, None, :]
    )
    owned_pages = jnp.any(page_match, axis=1)
    page_taken = jnp.any(owned_pages, axis=0)
    page_owner = jnp.sum(
        owned_pages.astype(jnp.int32) * jnp.arange(row_count, dtype=jnp.int32)[:, None], axis=0
    )
    page_start = jnp.sum(
        page_match.astype(jnp.int32)
        * (jnp.arange(max_pages, dtype=jnp.int32) * page_len)[None, :, None],
        axis=(0, 1),
    )
    page_limit = cache_length[page_owner]
    in_range = page_taken[:, None] & (
        page_start[:, None] + jnp.arange(page_len)[None, :] < page_limit[:, None]
    )
    queries = lax.all_to_all(queries_far, "req", split_axis=0, concat_axis=0, tiled=True)
    queries = (
        queries.reshape(experts, heads_here, capacity, head_dim)
        .transpose(0, 2, 1, 3)
        .reshape(experts * capacity, heads_here, head_dim)
    )
    page_slots = target.reshape(row_count, choices_each)[page_owner]
    key_page = key_new[page_owner]
    value_page = value_new[page_owner]
    same_owner = (
        page_taken[:, None] & page_taken[None, :] & (page_owner[:, None] == page_owner[None, :])
    )
    leader = jnp.any(local_ids[:, :1] == jnp.arange(pages_here)[None, :], axis=0)
    leader_float = leader.astype(jnp.float32)[:, None, None]
    page_raw = queries[page_slots]
    page_queries = rotate(page_raw.astype(jnp.float32), page_limit[:, None, None]).astype(
        jnp.bfloat16
    )
    score_scale = 1.0 / head_dim**0.5
    head_eye = jnp.eye(heads_here, dtype=jnp.bfloat16)
    spread_queries = page_queries[:, :, :, None, :] * head_eye[None, None, :, :, None]
    scores = (
        jnp.einsum(
            "pkjhd,pthd->pkjt", spread_queries, cache_keys, preferred_element_type=jnp.float32
        )
        * score_scale
    )
    scores = jnp.where(in_range[:, None, None, :], scores, -jnp.inf)
    fresh_score = (
        jnp.einsum("pkhd,phd->pkh", page_queries, key_page, preferred_element_type=jnp.float32)
        * score_scale
    )
    page_top = jnp.max(scores, axis=3)
    owner_top = jnp.max(jnp.where(same_owner[:, :, None, None], page_top[None], -jnp.inf), axis=1)
    row_top = jnp.maximum(owner_top, fresh_score)
    weights = jnp.exp(scores - row_top[..., None])
    fresh_weight = jnp.exp(fresh_score - row_top)
    owned_float = owned_pages.astype(jnp.float32)
    denominator = jnp.einsum(
        "rp,pkh->rkh",
        owned_float,
        jnp.sum(weights, axis=3) + leader_float * fresh_weight,
        precision=lax.Precision.HIGHEST,
    )
    weights_rounded = weights.astype(jnp.bfloat16)
    fresh_rounded = lax.optimization_barrier(fresh_weight.astype(jnp.bfloat16)).astype(jnp.float32)
    page_context = jnp.einsum(
        "pkjt,pthd->pkjhd", weights_rounded, cache_values, preferred_element_type=jnp.float32
    )
    page_context = jnp.sum(page_context * head_eye.astype(jnp.float32)[None, None, :, :, None], axis=3)
    page_context = page_context + (leader_float * fresh_rounded)[..., None] * value_page.astype(
        jnp.float32
    )[:, None]
    accumulated = jnp.einsum(
        "rp,pkhd->rkhd", owned_float, page_context, precision=lax.Precision.HIGHEST
    )
    context = (accumulated / denominator[..., None]).astype(jnp.bfloat16)
    context_flat = context.reshape(row_count * choices_each, heads_here * head_dim)
    context_buf = jnp.dot(select_rows, context_flat, preferred_element_type=jnp.float32).astype(
        jnp.bfloat16
    )
    context_buf = context_buf.reshape(experts, capacity, heads_here, head_dim).transpose(0, 2, 1, 3)
    context_buf = context_buf.reshape(groups, pairs_here, capacity, head_dim)
    head_count = lax.axis_size("head")
    width_here = model_width // head_count
    wblocks = width_here // lanes
    context_far = lax.all_to_all(context_buf, "req", split_axis=0, concat_axis=0, tiled=True)
    partial_far = jnp.dot(
        context_far.transpose(0, 2, 1, 3).reshape(groups * capacity, pairs_here * head_dim),
        output_weight.reshape(pairs_here * head_dim, model_width),
        preferred_element_type=jnp.float32,
    )
    partial_far = partial_far.reshape(groups, capacity, head_count, wblocks, lanes).transpose(
        0, 2, 1, 3, 4
    )
    gate_flat = expert_gate.reshape(-1)
    spread = (
        jnp.where(select, gate_flat[None, :], jnp.float32(0.0))
        .reshape(experts * capacity, row_count, choices_each)
        .sum(axis=2)
        .T
    )
    alive_rows = live_mask.astype(jnp.float32)[:, None]
    returned = lax.all_to_all(
        partial_far.reshape(groups * head_count, capacity * wblocks, lanes),
        ("req", "head"),
        split_axis=0,
        concat_axis=0,
        tiled=True,
    )
    summed = returned.reshape(experts, replicas * head_count, capacity * wblocks, lanes).sum(axis=1)
    result = jnp.einsum(
        "rm,mab->rab",
        spread,
        summed.reshape(experts * capacity, wblocks, lanes),
        precision=lax.Precision.HIGHEST,
    ).reshape(row_count, width_here)
    return (result * alive_rows).astype(jnp.bfloat16)


def solution(mesh):
    return jax.shard_map(
        body,
        mesh=mesh,
        in_specs=(
            P("req", None),
            P(),
            P(None, "head", None, None),
            P("req", None, "head"),
            P("req", "head", None),
            P("req", None, "head", None),
            P("req", None, "head", None),
            P("req"),
            P("req", None),
            P("req", None),
            P("req", None),
            P("req"),
        ),
        out_specs=P("req", "head"),
        check_vma=False,
    )
```

```python
import jax
import jax.numpy as jnp
from jax import lax
from jax.sharding import PartitionSpec as P

AEXP = 8
CAP = 12


eps = 1e-06
theta = 10000.0


def rotate(vectors, positions):
    half_width = vectors.shape[-1] // 2
    frequency = theta ** (-(jnp.arange(half_width, dtype=jnp.float32) * 2.0) / vectors.shape[-1])
    angles = positions.astype(jnp.float32)[..., None] * frequency
    cosine = jnp.cos(angles)
    sine_part = jnp.sin(angles)
    first_half = vectors[..., :half_width]
    second = vectors[..., half_width:]
    return jnp.concatenate(
        [first_half * cosine - second * sine_part, second * cosine + first_half * sine_part],
        axis=-1,
    )


def body(
    tokens,
    norm_gain,
    key_value_weight,
    query_weight,
    output_weight,
    cache_keys,
    cache_values,
    cache_length,
    page_table,
    expert_choice,
    expert_gate,
    live_mask,
):
    groups = lax.axis_size("req")
    group_index = lax.axis_index("req")
    row_count = tokens.shape[0]
    model_width = tokens.shape[1]
    choices_each = expert_choice.shape[1]
    heads_here = key_value_weight.shape[1]
    head_dim = key_value_weight.shape[3]
    pairs_here = query_weight.shape[0]
    pages_here = cache_keys.shape[0]
    page_len = cache_keys.shape[1]
    max_pages = page_table.shape[1]
    experts = AEXP
    capacity = CAP
    as_float = tokens.astype(jnp.float32)
    row_scale = lax.rsqrt(jnp.mean(as_float * as_float, axis=-1, keepdims=True) + eps)
    normed = (as_float * row_scale * norm_gain).astype(jnp.bfloat16)
    flat_expert = expert_choice.reshape(-1)
    onehot = (flat_expert[:, None] == jnp.arange(experts)[None, :]).astype(jnp.int32)
    before = jnp.cumsum(onehot, axis=0) - onehot
    slot_index = jnp.sum(before * onehot, axis=1)
    target = flat_expert * capacity + slot_index
    select = target[None, :] == jnp.arange(experts * capacity)[:, None]
    select_rows = select.astype(jnp.bfloat16)
    lanes = 128
    blocks = model_width // lanes
    repeated = jnp.repeat(tokens, choices_each, axis=0).reshape(-1, blocks, lanes)
    picked = jnp.einsum("mr,rab->mab", select_rows, repeated, preferred_element_type=jnp.float32)
    slot_scale = jnp.sum(
        jnp.where(select, jnp.repeat(row_scale[:, 0], choices_each)[None, :], jnp.float32(0.0)),
        axis=1,
    )
    sendbuf = (
        picked * slot_scale[:, None, None] * norm_gain.reshape(blocks, lanes)[None]
    ).astype(jnp.bfloat16)
    replicas = groups // experts
    sendbuf = jnp.broadcast_to(
        sendbuf.reshape(experts, 1, capacity, blocks, lanes),
        (experts, replicas, capacity, blocks, lanes),
    )
    sendbuf = sendbuf.reshape(groups, capacity * blocks, lanes)
    tokens_far = lax.all_to_all(sendbuf, "req", split_axis=0, concat_axis=0, tiled=True)
    queries_far = jnp.einsum(
        "snab,pabh->spnh",
        tokens_far.reshape(groups, capacity, blocks, lanes),
        query_weight.reshape(pairs_here, blocks, lanes, head_dim),
        preferred_element_type=jnp.float32,
    ).astype(jnp.bfloat16)
    key_value = jnp.einsum(
        "rf,fhkd->rhkd", normed, key_value_weight, preferred_element_type=jnp.float32
    )
    key_new = rotate(key_value[:, :, 0], cache_length[:, None]).astype(jnp.bfloat16)
    value_new = key_value[:, :, 1].astype(jnp.bfloat16)
    local_ids = page_table - group_index * pages_here
    page_used = jnp.arange(max_pages)[None, :] * page_len < cache_length[:, None]
    page_match = page_used[:, :, None] & (
        local_ids[:, :, None] == jnp.arange(pages_here)[None, None, :]
    )
    owned_pages = jnp.any(page_match, axis=1)
    page_taken = jnp.any(owned_pages, axis=0)
    page_owner = jnp.sum(
        owned_pages.astype(jnp.int32) * jnp.arange(row_count, dtype=jnp.int32)[:, None], axis=0
    )
    page_start = jnp.sum(
        page_match.astype(jnp.int32)
        * (jnp.arange(max_pages, dtype=jnp.int32) * page_len)[None, :, None],
        axis=(0, 1),
    )
    page_limit = cache_length[page_owner]
    in_range = page_taken[:, None] & (
        page_start[:, None] + jnp.arange(page_len)[None, :] < page_limit[:, None]
    )
    queries = lax.all_to_all(queries_far, "req", split_axis=0, concat_axis=0, tiled=True)
    queries = (
        queries.reshape(experts, heads_here, capacity, head_dim)
        .transpose(0, 2, 1, 3)
        .reshape(experts * capacity, heads_here, head_dim)
    )
    page_slots = target.reshape(row_count, choices_each)[page_owner]
    key_page = key_new[page_owner]
    value_page = value_new[page_owner]
    same_owner = (
        page_taken[:, None] & page_taken[None, :] & (page_owner[:, None] == page_owner[None, :])
    )
    leader = jnp.any(local_ids[:, :1] == jnp.arange(pages_here)[None, :], axis=0)
    leader_float = leader.astype(jnp.float32)[:, None, None]
    page_raw = queries[page_slots]
    page_queries = rotate(page_raw.astype(jnp.float32), page_limit[:, None, None]).astype(
        jnp.bfloat16
    )
    score_scale = 1.0 / head_dim**0.5
    head_eye = jnp.eye(heads_here, dtype=jnp.bfloat16)
    spread_queries = page_queries[:, :, :, None, :] * head_eye[None, None, :, :, None]
    scores = (
        jnp.einsum(
            "pkjhd,pthd->pkjt", spread_queries, cache_keys, preferred_element_type=jnp.float32
        )
        * score_scale
    )
    scores = jnp.where(in_range[:, None, None, :], scores, -jnp.inf)
    fresh_score = (
        jnp.einsum("pkhd,phd->pkh", page_queries, key_page, preferred_element_type=jnp.float32)
        * score_scale
    )
    page_top = jnp.max(scores, axis=3)
    owner_top = jnp.max(jnp.where(same_owner[:, :, None, None], page_top[None], -jnp.inf), axis=1)
    row_top = jnp.maximum(owner_top, fresh_score)
    weights = jnp.exp(scores - row_top[..., None])
    fresh_weight = jnp.exp(fresh_score - row_top)
    owned_float = owned_pages.astype(jnp.float32)
    denominator = jnp.einsum(
        "rp,pkh->rkh",
        owned_float,
        jnp.sum(weights, axis=3) + leader_float * fresh_weight,
        precision=lax.Precision.HIGHEST,
    )
    weights_rounded = weights.astype(jnp.bfloat16)
    fresh_rounded = lax.optimization_barrier(fresh_weight.astype(jnp.bfloat16)).astype(jnp.float32)
    page_context = jnp.einsum(
        "pkjt,pthd->pkjhd", weights_rounded, cache_values, preferred_element_type=jnp.float32
    )
    page_context = jnp.sum(page_context * head_eye.astype(jnp.float32)[None, None, :, :, None], axis=3)
    page_context = page_context + (leader_float * fresh_rounded)[..., None] * value_page.astype(
        jnp.float32
    )[:, None]
    accumulated = jnp.einsum(
        "rp,pkhd->rkhd", owned_float, page_context, precision=lax.Precision.HIGHEST
    )
    context = (accumulated / denominator[..., None]).astype(jnp.bfloat16)
    context_flat = context.reshape(row_count * choices_each, heads_here * head_dim)
    context_buf = jnp.dot(select_rows, context_flat, preferred_element_type=jnp.float32).astype(
        jnp.bfloat16
    )
    context_buf = context_buf.reshape(experts, capacity, heads_here, head_dim).transpose(0, 2, 1, 3)
    context_buf = context_buf.reshape(groups, pairs_here, capacity, head_dim)
    head_count = lax.axis_size("head")
    width_here = model_width // head_count
    wblocks = width_here // lanes
    partial_far = jnp.einsum(
        "spnh,phd->snd",
        lax.all_to_all(context_buf, "req", split_axis=0, concat_axis=0, tiled=True),
        output_weight,
        preferred_element_type=jnp.float32,
    )
    partial_far = partial_far.reshape(groups, capacity, head_count, wblocks, lanes).transpose(
        0, 2, 1, 3, 4
    )
    gate_flat = expert_gate.reshape(-1)
    spread = (
        jnp.where(select, gate_flat[None, :], jnp.float32(0.0))
        .reshape(experts * capacity, row_count, choices_each)
        .sum(axis=2)
        .T
    )
    alive_rows = live_mask.astype(jnp.float32)[:, None]
    returned = lax.all_to_all(
        partial_far.reshape(groups * head_count, capacity * wblocks, lanes),
        ("req", "head"),
        split_axis=0,
        concat_axis=0,
        tiled=True,
    )
    summed = returned.reshape(experts, replicas * head_count, capacity * wblocks, lanes).sum(axis=1)
    result = jnp.einsum(
        "rm,mab->rab",
        spread,
        summed.reshape(experts * capacity, wblocks, lanes),
        precision=lax.Precision.HIGHEST,
    ).reshape(row_count, width_here)
    return (result * alive_rows).astype(jnp.bfloat16)


def solution(mesh):
    return jax.shard_map(
        body,
        mesh=mesh,
        in_specs=(
            P("req", None),
            P(),
            P(None, "head", None, None),
            P("req", None, "head"),
            P("req", "head", None),
            P("req", None, "head", None),
            P("req", None, "head", None),
            P("req"),
            P("req", None),
            P("req", None),
            P("req", None),
            P("req"),
        ),
        out_specs=P("req", "head"),
        check_vma=False,
    )
```

```python
import jax
import jax.numpy as jnp
from jax import lax
from jax.experimental import pallas as pl
from jax.sharding import PartitionSpec as P

AEXP = 8
CAP = 12


eps = 1e-06
theta = 10000.0


def rotate(vectors, positions):
    half_width = vectors.shape[-1] // 2
    frequency = theta ** (-(jnp.arange(half_width, dtype=jnp.float32) * 2.0) / vectors.shape[-1])
    angles = positions.astype(jnp.float32)[..., None] * frequency
    cosine = jnp.cos(angles)
    sine_part = jnp.sin(angles)
    first_half = vectors[..., :half_width]
    second = vectors[..., half_width:]
    return jnp.concatenate(
        [first_half * cosine - second * sine_part, second * cosine + first_half * sine_part],
        axis=-1,
    )


def norm_kernel(tokens_ref, gain_ref, out_ref):
    as_float = tokens_ref[...].astype(jnp.float32)
    mean_square = jnp.mean(as_float * as_float, axis=-1, keepdims=True)
    out_ref[...] = (as_float * lax.rsqrt(mean_square + eps) * gain_ref[...]).astype(out_ref.dtype)


def body(
    tokens,
    norm_gain,
    key_value_weight,
    query_weight,
    output_weight,
    cache_keys,
    cache_values,
    cache_length,
    page_table,
    expert_choice,
    expert_gate,
    live_mask,
):
    groups = lax.axis_size("req")
    group_index = lax.axis_index("req")
    row_count = tokens.shape[0]
    model_width = tokens.shape[1]
    choices_each = expert_choice.shape[1]
    heads_here = key_value_weight.shape[1]
    head_dim = key_value_weight.shape[3]
    pairs_here = query_weight.shape[0]
    pages_here = cache_keys.shape[0]
    page_len = cache_keys.shape[1]
    max_pages = page_table.shape[1]
    experts = AEXP
    capacity = CAP
    normed = pl.pallas_call(
        norm_kernel, out_shape=jax.ShapeDtypeStruct(tokens.shape, jnp.bfloat16)
    )(tokens, norm_gain.reshape(1, -1))
    flat_expert = expert_choice.reshape(-1)
    onehot = (flat_expert[:, None] == jnp.arange(experts)[None, :]).astype(jnp.int32)
    before = jnp.cumsum(onehot, axis=0) - onehot
    slot_index = jnp.sum(before * onehot, axis=1)
    target = flat_expert * capacity + slot_index
    select = target[None, :] == jnp.arange(experts * capacity)[:, None]
    select_rows = select.astype(jnp.bfloat16)
    lanes = 128
    blocks = model_width // lanes
    repeated = jnp.repeat(normed, choices_each, axis=0).reshape(-1, blocks, lanes)
    sendbuf = jnp.einsum(
        "mr,rab->mab", select_rows, repeated, preferred_element_type=jnp.float32
    ).astype(jnp.bfloat16)
    replicas = groups // experts
    sendbuf = jnp.broadcast_to(
        sendbuf.reshape(experts, 1, capacity, blocks, lanes),
        (experts, replicas, capacity, blocks, lanes),
    )
    sendbuf = sendbuf.reshape(groups, capacity * blocks, lanes)
    tokens_far = lax.all_to_all(sendbuf, "req", split_axis=0, concat_axis=0, tiled=True)
    queries_far = jnp.einsum(
        "snab,pabh->spnh",
        tokens_far.reshape(groups, capacity, blocks, lanes),
        query_weight.reshape(pairs_here, blocks, lanes, head_dim),
        preferred_element_type=jnp.float32,
    ).astype(jnp.bfloat16)
    key_value = jnp.einsum(
        "rf,fhkd->rhkd", normed, key_value_weight, preferred_element_type=jnp.float32
    )
    key_new = rotate(key_value[:, :, 0], cache_length[:, None]).astype(jnp.bfloat16)
    value_new = key_value[:, :, 1].astype(jnp.bfloat16)
    local_ids = page_table - group_index * pages_here
    page_used = jnp.arange(max_pages)[None, :] * page_len < cache_length[:, None]
    page_match = page_used[:, :, None] & (
        local_ids[:, :, None] == jnp.arange(pages_here)[None, None, :]
    )
    owned_pages = jnp.any(page_match, axis=1)
    page_taken = jnp.any(owned_pages, axis=0)
    page_owner = jnp.sum(
        owned_pages.astype(jnp.int32) * jnp.arange(row_count, dtype=jnp.int32)[:, None], axis=0
    )
    page_start = jnp.sum(
        page_match.astype(jnp.int32)
        * (jnp.arange(max_pages, dtype=jnp.int32) * page_len)[None, :, None],
        axis=(0, 1),
    )
    page_limit = cache_length[page_owner]
    in_range = page_taken[:, None] & (
        page_start[:, None] + jnp.arange(page_len)[None, :] < page_limit[:, None]
    )
    queries = lax.all_to_all(queries_far, "req", split_axis=0, concat_axis=0, tiled=True)
    queries = (
        queries.reshape(experts, heads_here, capacity, head_dim)
        .transpose(0, 2, 1, 3)
        .reshape(experts * capacity, heads_here, head_dim)
    )
    page_slots = target.reshape(row_count, choices_each)[page_owner]
    key_page = key_new[page_owner]
    value_page = value_new[page_owner]
    same_owner = (
        page_taken[:, None] & page_taken[None, :] & (page_owner[:, None] == page_owner[None, :])
    )
    leader = jnp.any(local_ids[:, :1] == jnp.arange(pages_here)[None, :], axis=0)
    leader_float = leader.astype(jnp.float32)[:, None, None]
    page_raw = queries[page_slots]
    page_queries = rotate(page_raw.astype(jnp.float32), page_limit[:, None, None]).astype(
        jnp.bfloat16
    )
    score_scale = 1.0 / head_dim**0.5
    head_eye = jnp.eye(heads_here, dtype=jnp.bfloat16)
    spread_queries = page_queries[:, :, :, None, :] * head_eye[None, None, :, :, None]
    scores = (
        jnp.einsum(
            "pkjhd,pthd->pkjt", spread_queries, cache_keys, preferred_element_type=jnp.float32
        )
        * score_scale
    )
    scores = jnp.where(in_range[:, None, None, :], scores, -jnp.inf)
    fresh_score = (
        jnp.einsum("pkhd,phd->pkh", page_queries, key_page, preferred_element_type=jnp.float32)
        * score_scale
    )
    page_top = jnp.max(scores, axis=3)
    owner_top = jnp.max(jnp.where(same_owner[:, :, None, None], page_top[None], -jnp.inf), axis=1)
    row_top = jnp.maximum(owner_top, fresh_score)
    weights = jnp.exp(scores - row_top[..., None])
    fresh_weight = jnp.exp(fresh_score - row_top)
    owned_float = owned_pages.astype(jnp.float32)
    denominator = jnp.einsum(
        "rp,pkh->rkh",
        owned_float,
        jnp.sum(weights, axis=3) + leader_float * fresh_weight,
        precision=lax.Precision.HIGHEST,
    )
    weights_rounded = weights.astype(jnp.bfloat16)
    fresh_rounded = lax.optimization_barrier(fresh_weight.astype(jnp.bfloat16)).astype(jnp.float32)
    page_context = jnp.einsum(
        "pkjt,pthd->pkjhd", weights_rounded, cache_values, preferred_element_type=jnp.float32
    )
    page_context = jnp.sum(page_context * head_eye.astype(jnp.float32)[None, None, :, :, None], axis=3)
    page_context = page_context + (leader_float * fresh_rounded)[..., None] * value_page.astype(
        jnp.float32
    )[:, None]
    accumulated = jnp.einsum(
        "rp,pkhd->rkhd", owned_float, page_context, precision=lax.Precision.HIGHEST
    )
    context = (accumulated / denominator[..., None]).astype(jnp.bfloat16)
    context_flat = context.reshape(row_count * choices_each, heads_here * head_dim)
    context_buf = jnp.dot(select_rows, context_flat, preferred_element_type=jnp.float32).astype(
        jnp.bfloat16
    )
    context_buf = context_buf.reshape(experts, capacity, heads_here, head_dim).transpose(0, 2, 1, 3)
    context_buf = context_buf.reshape(groups, pairs_here, capacity, head_dim)
    head_count = lax.axis_size("head")
    width_here = model_width // head_count
    wblocks = width_here // lanes
    partial_far = jnp.einsum(
        "spnh,phd->snd",
        lax.all_to_all(context_buf, "req", split_axis=0, concat_axis=0, tiled=True),
        output_weight,
        preferred_element_type=jnp.float32,
    )
    partial_far = partial_far.reshape(groups, capacity, head_count, wblocks, lanes).transpose(
        0, 2, 1, 3, 4
    )
    gate_flat = expert_gate.reshape(-1)
    spread = (
        jnp.where(select, gate_flat[None, :], jnp.float32(0.0))
        .reshape(experts * capacity, row_count, choices_each)
        .sum(axis=2)
        .T
    )
    alive_rows = live_mask.astype(jnp.float32)[:, None]
    returned = lax.all_to_all(
        partial_far.reshape(groups * head_count, capacity * wblocks, lanes),
        ("req", "head"),
        split_axis=0,
        concat_axis=0,
        tiled=True,
    )
    summed = returned.reshape(experts, replicas * head_count, capacity * wblocks, lanes).sum(axis=1)
    result = jnp.einsum(
        "rm,mab->rab",
        spread,
        summed.reshape(experts * capacity, wblocks, lanes),
        precision=lax.Precision.HIGHEST,
    ).reshape(row_count, width_here)
    return (result * alive_rows).astype(jnp.bfloat16)


def solution(mesh):
    return jax.shard_map(
        body,
        mesh=mesh,
        in_specs=(
            P("req", None),
            P(),
            P(None, "head", None, None),
            P("req", None, "head"),
            P("req", "head", None),
            P("req", None, "head", None),
            P("req", None, "head", None),
            P("req"),
            P("req", None),
            P("req", None),
            P("req", None),
            P("req"),
        ),
        out_specs=P("req", "head"),
        check_vma=False,
    )
```

```python
import jax
import jax.numpy as jnp
from jax import lax
from jax.experimental import pallas as pl
from jax.sharding import PartitionSpec as P

AEXP = 8
CAP = 12


eps = 1e-06
theta = 10000.0


def rotate(vectors, positions):
    half_width = vectors.shape[-1] // 2
    frequency = theta ** (-(jnp.arange(half_width, dtype=jnp.float32) * 2.0) / vectors.shape[-1])
    angles = positions.astype(jnp.float32)[..., None] * frequency
    cosine = jnp.cos(angles)
    sine_part = jnp.sin(angles)
    first_half = vectors[..., :half_width]
    second = vectors[..., half_width:]
    return jnp.concatenate(
        [first_half * cosine - second * sine_part, second * cosine + first_half * sine_part],
        axis=-1,
    )


def norm_kernel(tokens_ref, gain_ref, out_ref):
    as_float = tokens_ref[...].astype(jnp.float32)
    mean_square = jnp.mean(as_float * as_float, axis=-1, keepdims=True)
    out_ref[...] = (as_float * lax.rsqrt(mean_square + eps) * gain_ref[...]).astype(out_ref.dtype)


def body(
    tokens,
    norm_gain,
    key_value_weight,
    query_weight,
    output_weight,
    cache_keys,
    cache_values,
    cache_length,
    page_table,
    expert_choice,
    expert_gate,
    live_mask,
):
    groups = lax.axis_size("req")
    group_index = lax.axis_index("req")
    row_count = tokens.shape[0]
    model_width = tokens.shape[1]
    choices_each = expert_choice.shape[1]
    heads_here = key_value_weight.shape[1]
    head_dim = key_value_weight.shape[3]
    pairs_here = query_weight.shape[0]
    pages_here = cache_keys.shape[0]
    page_len = cache_keys.shape[1]
    max_pages = page_table.shape[1]
    experts = AEXP
    capacity = CAP
    normed = pl.pallas_call(
        norm_kernel, out_shape=jax.ShapeDtypeStruct(tokens.shape, jnp.bfloat16)
    )(tokens, norm_gain.reshape(1, -1))
    flat_expert = expert_choice.reshape(-1)
    onehot = (flat_expert[:, None] == jnp.arange(experts)[None, :]).astype(jnp.int32)
    before = jnp.cumsum(onehot, axis=0) - onehot
    slot_index = jnp.sum(before * onehot, axis=1)
    target = flat_expert * capacity + slot_index
    select = target[None, :] == jnp.arange(experts * capacity)[:, None]
    select_rows = select.astype(jnp.bfloat16)
    lanes = 128
    blocks = model_width // lanes
    select_tokens = jnp.any(
        select.reshape(experts * capacity, row_count, choices_each), axis=2
    ).astype(jnp.bfloat16)
    sendbuf = jnp.einsum(
        "mr,rab->mab",
        select_tokens,
        normed.reshape(row_count, blocks, lanes),
        preferred_element_type=jnp.float32,
    ).astype(jnp.bfloat16)
    replicas = groups // experts
    sendbuf = jnp.broadcast_to(
        sendbuf.reshape(experts, 1, capacity, blocks, lanes),
        (experts, replicas, capacity, blocks, lanes),
    )
    sendbuf = sendbuf.reshape(groups, capacity * blocks, lanes)
    tokens_far = lax.all_to_all(sendbuf, "req", split_axis=0, concat_axis=0, tiled=True)
    queries_far = jnp.einsum(
        "snab,pabh->spnh",
        tokens_far.reshape(groups, capacity, blocks, lanes),
        query_weight.reshape(pairs_here, blocks, lanes, head_dim),
        preferred_element_type=jnp.float32,
    ).astype(jnp.bfloat16)
    key_value = jnp.einsum(
        "rf,fhkd->rhkd", normed, key_value_weight, preferred_element_type=jnp.float32
    )
    key_new = rotate(key_value[:, :, 0], cache_length[:, None]).astype(jnp.bfloat16)
    value_new = key_value[:, :, 1].astype(jnp.bfloat16)
    local_ids = page_table - group_index * pages_here
    page_used = jnp.arange(max_pages)[None, :] * page_len < cache_length[:, None]
    page_match = page_used[:, :, None] & (
        local_ids[:, :, None] == jnp.arange(pages_here)[None, None, :]
    )
    owned_pages = jnp.any(page_match, axis=1)
    page_taken = jnp.any(owned_pages, axis=0)
    page_owner = jnp.sum(
        owned_pages.astype(jnp.int32) * jnp.arange(row_count, dtype=jnp.int32)[:, None], axis=0
    )
    page_start = jnp.sum(
        page_match.astype(jnp.int32)
        * (jnp.arange(max_pages, dtype=jnp.int32) * page_len)[None, :, None],
        axis=(0, 1),
    )
    page_limit = cache_length[page_owner]
    in_range = page_taken[:, None] & (
        page_start[:, None] + jnp.arange(page_len)[None, :] < page_limit[:, None]
    )
    queries = lax.all_to_all(queries_far, "req", split_axis=0, concat_axis=0, tiled=True)
    queries = (
        queries.reshape(experts, heads_here, capacity, head_dim)
        .transpose(0, 2, 1, 3)
        .reshape(experts * capacity, heads_here, head_dim)
    )
    page_slots = target.reshape(row_count, choices_each)[page_owner]
    key_page = key_new[page_owner]
    value_page = value_new[page_owner]
    same_owner = (
        page_taken[:, None] & page_taken[None, :] & (page_owner[:, None] == page_owner[None, :])
    )
    leader = jnp.any(local_ids[:, :1] == jnp.arange(pages_here)[None, :], axis=0)
    leader_float = leader.astype(jnp.float32)[:, None, None]
    page_raw = queries[page_slots]
    page_queries = rotate(page_raw.astype(jnp.float32), page_limit[:, None, None]).astype(
        jnp.bfloat16
    )
    score_scale = 1.0 / head_dim**0.5
    head_eye = jnp.eye(heads_here, dtype=jnp.bfloat16)
    spread_queries = page_queries[:, :, :, None, :] * head_eye[None, None, :, :, None]
    scores = (
        jnp.einsum(
            "pkjhd,pthd->pkjt", spread_queries, cache_keys, preferred_element_type=jnp.float32
        )
        * score_scale
    )
    scores = jnp.where(in_range[:, None, None, :], scores, -jnp.inf)
    fresh_score = (
        jnp.einsum("pkhd,phd->pkh", page_queries, key_page, preferred_element_type=jnp.float32)
        * score_scale
    )
    page_top = jnp.max(scores, axis=3)
    owner_top = jnp.max(jnp.where(same_owner[:, :, None, None], page_top[None], -jnp.inf), axis=1)
    row_top = jnp.maximum(owner_top, fresh_score)
    weights = jnp.exp(scores - row_top[..., None])
    fresh_weight = jnp.exp(fresh_score - row_top)
    owned_float = owned_pages.astype(jnp.float32)
    denominator = jnp.einsum(
        "rp,pkh->rkh",
        owned_float,
        jnp.sum(weights, axis=3) + leader_float * fresh_weight,
        precision=lax.Precision.HIGHEST,
    )
    weights_rounded = weights.astype(jnp.bfloat16)
    fresh_rounded = lax.optimization_barrier(fresh_weight.astype(jnp.bfloat16)).astype(jnp.float32)
    page_context = jnp.einsum(
        "pkjt,pthd->pkjhd", weights_rounded, cache_values, preferred_element_type=jnp.float32
    )
    page_context = jnp.sum(page_context * head_eye.astype(jnp.float32)[None, None, :, :, None], axis=3)
    page_context = page_context + (leader_float * fresh_rounded)[..., None] * value_page.astype(
        jnp.float32
    )[:, None]
    accumulated = jnp.einsum(
        "rp,pkhd->rkhd", owned_float, page_context, precision=lax.Precision.HIGHEST
    )
    context = (accumulated / denominator[..., None]).astype(jnp.bfloat16)
    context_flat = context.reshape(row_count * choices_each, heads_here * head_dim)
    context_buf = jnp.dot(select_rows, context_flat, preferred_element_type=jnp.float32).astype(
        jnp.bfloat16
    )
    context_buf = context_buf.reshape(experts, capacity, heads_here, head_dim).transpose(0, 2, 1, 3)
    context_buf = context_buf.reshape(groups, pairs_here, capacity, head_dim)
    head_count = lax.axis_size("head")
    width_here = model_width // head_count
    wblocks = width_here // lanes
    partial_far = jnp.einsum(
        "spnh,phd->snd",
        lax.all_to_all(context_buf, "req", split_axis=0, concat_axis=0, tiled=True),
        output_weight,
        preferred_element_type=jnp.float32,
    )
    partial_far = partial_far.reshape(groups, capacity, head_count, wblocks, lanes).transpose(
        0, 2, 1, 3, 4
    )
    gate_flat = expert_gate.reshape(-1)
    spread = (
        jnp.where(select, gate_flat[None, :], jnp.float32(0.0))
        .reshape(experts * capacity, row_count, choices_each)
        .sum(axis=2)
        .T
    )
    alive_rows = live_mask.astype(jnp.float32)[:, None]
    returned = lax.all_to_all(
        partial_far.reshape(groups * head_count, capacity * wblocks, lanes),
        ("req", "head"),
        split_axis=0,
        concat_axis=0,
        tiled=True,
    )
    summed = returned.reshape(experts, replicas * head_count, capacity * wblocks, lanes).sum(axis=1)
    result = jnp.einsum(
        "rm,mab->rab",
        spread,
        summed.reshape(experts * capacity, wblocks, lanes),
        precision=lax.Precision.HIGHEST,
    ).reshape(row_count, width_here)
    return (result * alive_rows).astype(jnp.bfloat16)


def solution(mesh):
    return jax.shard_map(
        body,
        mesh=mesh,
        in_specs=(
            P("req", None),
            P(),
            P(None, "head", None, None),
            P("req", None, "head"),
            P("req", "head", None),
            P("req", None, "head", None),
            P("req", None, "head", None),
            P("req"),
            P("req", None),
            P("req", None),
            P("req", None),
            P("req"),
        ),
        out_specs=P("req", "head"),
        check_vma=False,
    )
```

```python
import jax
import jax.numpy as jnp
from jax import lax
from jax.sharding import PartitionSpec as P

AEXP = 8
CAP = 12


eps = 1e-06
theta = 10000.0


def rotate(vectors, positions):
    half_width = vectors.shape[-1] // 2
    frequency = theta ** (-(jnp.arange(half_width, dtype=jnp.float32) * 2.0) / vectors.shape[-1])
    angles = positions.astype(jnp.float32)[..., None] * frequency
    cosine = jnp.cos(angles)
    sine_part = jnp.sin(angles)
    first_half = vectors[..., :half_width]
    second = vectors[..., half_width:]
    return jnp.concatenate(
        [first_half * cosine - second * sine_part, second * cosine + first_half * sine_part],
        axis=-1,
    )


def body(
    tokens,
    norm_gain,
    key_value_weight,
    query_weight,
    output_weight,
    cache_keys,
    cache_values,
    cache_length,
    page_table,
    expert_choice,
    expert_gate,
    live_mask,
):
    groups = lax.axis_size("req")
    group_index = lax.axis_index("req")
    row_count = tokens.shape[0]
    model_width = tokens.shape[1]
    choices_each = expert_choice.shape[1]
    heads_here = key_value_weight.shape[1]
    head_dim = key_value_weight.shape[3]
    pairs_here = query_weight.shape[0]
    pages_here = cache_keys.shape[0]
    page_len = cache_keys.shape[1]
    max_pages = page_table.shape[1]
    experts = AEXP
    capacity = CAP
    as_float = tokens.astype(jnp.float32)
    normed = (
        as_float
        * lax.rsqrt(jnp.mean(as_float * as_float, axis=-1, keepdims=True) + eps)
        * norm_gain
    ).astype(jnp.bfloat16)
    flat_expert = expert_choice.reshape(-1)
    onehot = (flat_expert[:, None] == jnp.arange(experts)[None, :]).astype(jnp.int32)
    before = jnp.cumsum(onehot, axis=0) - onehot
    slot_index = jnp.sum(before * onehot, axis=1)
    target = flat_expert * capacity + slot_index
    select = target[None, :] == jnp.arange(experts * capacity)[:, None]
    select_rows = select.astype(jnp.bfloat16)
    lanes = 128
    blocks = model_width // lanes
    select_tokens = jnp.any(
        select.reshape(experts * capacity, row_count, choices_each), axis=2
    ).astype(jnp.bfloat16)
    sendbuf = jnp.einsum(
        "mr,rab->mab",
        select_tokens,
        normed.reshape(row_count, blocks, lanes),
        preferred_element_type=jnp.float32,
    ).astype(jnp.bfloat16)
    replicas = groups // experts
    sendbuf = jnp.broadcast_to(
        sendbuf.reshape(experts, 1, capacity, blocks, lanes),
        (experts, replicas, capacity, blocks, lanes),
    )
    sendbuf = sendbuf.reshape(groups, capacity * blocks, lanes)
    tokens_far = lax.all_to_all(sendbuf, "req", split_axis=0, concat_axis=0, tiled=True)
    queries_far = jnp.einsum(
        "snab,pabh->spnh",
        tokens_far.reshape(groups, capacity, blocks, lanes),
        query_weight.reshape(pairs_here, blocks, lanes, head_dim),
        preferred_element_type=jnp.float32,
    ).astype(jnp.bfloat16)
    key_value = jnp.einsum(
        "rf,fhkd->rhkd", normed, key_value_weight, preferred_element_type=jnp.float32
    )
    key_new = rotate(key_value[:, :, 0], cache_length[:, None]).astype(jnp.bfloat16)
    value_new = key_value[:, :, 1].astype(jnp.bfloat16)
    local_ids = page_table - group_index * pages_here
    page_used = jnp.arange(max_pages)[None, :] * page_len < cache_length[:, None]
    page_match = page_used[:, :, None] & (
        local_ids[:, :, None] == jnp.arange(pages_here)[None, None, :]
    )
    owned_pages = jnp.any(page_match, axis=1)
    page_taken = jnp.any(owned_pages, axis=0)
    page_owner = jnp.sum(
        owned_pages.astype(jnp.int32) * jnp.arange(row_count, dtype=jnp.int32)[:, None], axis=0
    )
    page_start = jnp.sum(
        page_match.astype(jnp.int32)
        * (jnp.arange(max_pages, dtype=jnp.int32) * page_len)[None, :, None],
        axis=(0, 1),
    )
    page_limit = cache_length[page_owner]
    in_range = page_taken[:, None] & (
        page_start[:, None] + jnp.arange(page_len)[None, :] < page_limit[:, None]
    )
    queries = lax.all_to_all(queries_far, "req", split_axis=0, concat_axis=0, tiled=True)
    queries = (
        queries.reshape(experts, heads_here, capacity, head_dim)
        .transpose(0, 2, 1, 3)
        .reshape(experts * capacity, heads_here, head_dim)
    )
    page_slots = target.reshape(row_count, choices_each)[page_owner]
    key_page = key_new[page_owner]
    value_page = value_new[page_owner]
    same_owner = (
        page_taken[:, None] & page_taken[None, :] & (page_owner[:, None] == page_owner[None, :])
    )
    leader = jnp.any(local_ids[:, :1] == jnp.arange(pages_here)[None, :], axis=0)
    leader_float = leader.astype(jnp.float32)[:, None, None]
    page_raw = queries[page_slots]
    page_queries = rotate(page_raw.astype(jnp.float32), page_limit[:, None, None]).astype(
        jnp.bfloat16
    )
    score_scale = 1.0 / head_dim**0.5
    head_eye = jnp.eye(heads_here, dtype=jnp.bfloat16)
    spread_queries = page_queries[:, :, :, None, :] * head_eye[None, None, :, :, None]
    scores = (
        jnp.einsum(
            "pkjhd,pthd->pkjt", spread_queries, cache_keys, preferred_element_type=jnp.float32
        )
        * score_scale
    )
    scores = jnp.where(in_range[:, None, None, :], scores, -jnp.inf)
    fresh_score = (
        jnp.einsum("pkhd,phd->pkh", page_queries, key_page, preferred_element_type=jnp.float32)
        * score_scale
    )
    page_top = jnp.max(scores, axis=3)
    owner_top = jnp.max(jnp.where(same_owner[:, :, None, None], page_top[None], -jnp.inf), axis=1)
    row_top = jnp.maximum(owner_top, fresh_score)
    weights = jnp.exp(scores - row_top[..., None])
    fresh_weight = jnp.exp(fresh_score - row_top)
    owned_float = owned_pages.astype(jnp.float32)
    denominator = jnp.einsum(
        "rp,pkh->rkh",
        owned_float,
        jnp.sum(weights, axis=3) + leader_float * fresh_weight,
        precision=lax.Precision.HIGHEST,
    )
    weights_rounded = weights.astype(jnp.bfloat16)
    fresh_rounded = lax.optimization_barrier(fresh_weight.astype(jnp.bfloat16)).astype(jnp.float32)
    page_context = jnp.einsum(
        "pkjt,pthd->pkjhd", weights_rounded, cache_values, preferred_element_type=jnp.float32
    )
    page_context = jnp.sum(page_context * head_eye.astype(jnp.float32)[None, None, :, :, None], axis=3)
    page_context = page_context + (leader_float * fresh_rounded)[..., None] * value_page.astype(
        jnp.float32
    )[:, None]
    accumulated = jnp.einsum(
        "rp,pkhd->rkhd", owned_float, page_context, precision=lax.Precision.HIGHEST
    )
    context = (accumulated / denominator[..., None]).astype(jnp.bfloat16)
    context_flat = context.reshape(row_count * choices_each, heads_here * head_dim)
    context_buf = jnp.dot(select_rows, context_flat, preferred_element_type=jnp.float32).astype(
        jnp.bfloat16
    )
    context_buf = context_buf.reshape(experts, capacity, heads_here, head_dim).transpose(0, 2, 1, 3)
    context_buf = context_buf.reshape(groups, pairs_here, capacity, head_dim)
    head_count = lax.axis_size("head")
    width_here = model_width // head_count
    wblocks = width_here // lanes
    partial_far = jnp.einsum(
        "spnh,phd->snd",
        lax.all_to_all(context_buf, "req", split_axis=0, concat_axis=0, tiled=True),
        output_weight,
        preferred_element_type=jnp.float32,
    )
    partial_far = partial_far.reshape(groups, capacity, head_count, wblocks, lanes).transpose(
        0, 2, 1, 3, 4
    )
    gate_flat = expert_gate.reshape(-1)
    spread = (
        jnp.where(select, gate_flat[None, :], jnp.float32(0.0))
        .reshape(experts * capacity, row_count, choices_each)
        .sum(axis=2)
        .T
    )
    alive_rows = live_mask.astype(jnp.float32)[:, None]
    returned = lax.all_to_all(
        partial_far.reshape(groups * head_count, capacity * wblocks, lanes),
        ("req", "head"),
        split_axis=0,
        concat_axis=0,
        tiled=True,
    )
    summed = returned.reshape(experts, replicas * head_count, capacity * wblocks, lanes).sum(axis=1)
    result = jnp.einsum(
        "rm,mab->rab",
        spread,
        summed.reshape(experts * capacity, wblocks, lanes),
        precision=lax.Precision.HIGHEST,
    ).reshape(row_count, width_here)
    return (result * alive_rows).astype(jnp.bfloat16)


def solution(mesh):
    return jax.shard_map(
        body,
        mesh=mesh,
        in_specs=(
            P("req", None),
            P(),
            P(None, "head", None, None),
            P("req", None, "head"),
            P("req", "head", None),
            P("req", None, "head", None),
            P("req", None, "head", None),
            P("req"),
            P("req", None),
            P("req", None),
            P("req", None),
            P("req"),
        ),
        out_specs=P("req", "head"),
        check_vma=False,
    )
```

```python
import jax
import jax.numpy as jnp
from jax import lax
from jax.sharding import PartitionSpec as P

AEXP = 8
CAP = 12


eps = 1e-06
theta = 10000.0


def rotate(vectors, positions):
    half_width = vectors.shape[-1] // 2
    frequency = theta ** (-(jnp.arange(half_width, dtype=jnp.float32) * 2.0) / vectors.shape[-1])
    angles = positions.astype(jnp.float32)[..., None] * frequency
    cosine = jnp.cos(angles)
    sine_part = jnp.sin(angles)
    first_half = vectors[..., :half_width]
    second = vectors[..., half_width:]
    return jnp.concatenate(
        [first_half * cosine - second * sine_part, second * cosine + first_half * sine_part],
        axis=-1,
    )


def body(
    tokens,
    norm_gain,
    key_value_weight,
    query_weight,
    output_weight,
    cache_keys,
    cache_values,
    cache_length,
    page_table,
    expert_choice,
    expert_gate,
    live_mask,
):
    groups = lax.axis_size("req")
    group_index = lax.axis_index("req")
    row_count = tokens.shape[0]
    model_width = tokens.shape[1]
    choices_each = expert_choice.shape[1]
    heads_here = key_value_weight.shape[1]
    head_dim = key_value_weight.shape[3]
    pairs_here = query_weight.shape[0]
    pages_here = cache_keys.shape[0]
    page_len = cache_keys.shape[1]
    max_pages = page_table.shape[1]
    experts = AEXP
    capacity = CAP
    as_float = tokens.astype(jnp.float32)
    normed = (
        as_float
        * lax.rsqrt(jnp.mean(as_float * as_float, axis=-1, keepdims=True) + eps)
        * norm_gain
    ).astype(jnp.bfloat16)
    flat_expert = expert_choice.reshape(-1)
    onehot = (flat_expert[:, None] == jnp.arange(experts)[None, :]).astype(jnp.int32)
    before = jnp.cumsum(onehot, axis=0) - onehot
    slot_index = jnp.sum(before * onehot, axis=1)
    target = flat_expert * capacity + slot_index
    select = target[None, :] == jnp.arange(experts * capacity)[:, None]
    select_rows = select.astype(jnp.bfloat16)
    lanes = 128
    blocks = model_width // lanes
    repeated = jnp.repeat(normed, choices_each, axis=0).reshape(-1, blocks, lanes)
    sendbuf = jnp.einsum(
        "mr,rab->mab", select_rows, repeated, preferred_element_type=jnp.float32
    ).astype(jnp.bfloat16)
    replicas = groups // experts
    sendbuf = jnp.broadcast_to(
        sendbuf.reshape(experts, 1, capacity, blocks, lanes),
        (experts, replicas, capacity, blocks, lanes),
    )
    sendbuf = sendbuf.reshape(groups, capacity * blocks, lanes)
    tokens_far = lax.all_to_all(sendbuf, "req", split_axis=0, concat_axis=0, tiled=True)
    queries_far = jnp.einsum(
        "snab,pabh->spnh",
        tokens_far.reshape(groups, capacity, blocks, lanes),
        query_weight.reshape(pairs_here, blocks, lanes, head_dim),
        preferred_element_type=jnp.float32,
    ).astype(jnp.bfloat16)
    key_value = jnp.einsum(
        "rf,fhkd->rhkd", normed, key_value_weight, preferred_element_type=jnp.float32
    )
    key_new = rotate(key_value[:, :, 0], cache_length[:, None]).astype(jnp.bfloat16)
    value_new = key_value[:, :, 1].astype(jnp.bfloat16)
    local_ids = page_table - group_index * pages_here
    page_used = jnp.arange(max_pages)[None, :] * page_len < cache_length[:, None]
    page_match = page_used[:, :, None] & (
        local_ids[:, :, None] == jnp.arange(pages_here)[None, None, :]
    )
    owned_pages = jnp.any(page_match, axis=1)
    page_taken = jnp.any(owned_pages, axis=0)
    page_owner = jnp.sum(
        owned_pages.astype(jnp.int32) * jnp.arange(row_count, dtype=jnp.int32)[:, None], axis=0
    )
    page_start = jnp.sum(
        page_match.astype(jnp.int32)
        * (jnp.arange(max_pages, dtype=jnp.int32) * page_len)[None, :, None],
        axis=(0, 1),
    )
    page_limit = cache_length[page_owner]
    in_range = page_taken[:, None] & (
        page_start[:, None] + jnp.arange(page_len)[None, :] < page_limit[:, None]
    )
    queries = lax.all_to_all(queries_far, "req", split_axis=0, concat_axis=0, tiled=True)
    queries = (
        queries.reshape(experts, heads_here, capacity, head_dim)
        .transpose(0, 2, 1, 3)
        .reshape(experts * capacity, heads_here, head_dim)
    )
    page_slots = target.reshape(row_count, choices_each)[page_owner]
    key_page = key_new[page_owner]
    value_page = value_new[page_owner]
    same_owner = (
        page_taken[:, None] & page_taken[None, :] & (page_owner[:, None] == page_owner[None, :])
    )
    leader = jnp.any(local_ids[:, :1] == jnp.arange(pages_here)[None, :], axis=0)
    leader_float = leader.astype(jnp.float32)[:, None, None]
    page_raw = queries[page_slots]
    page_queries = rotate(page_raw.astype(jnp.float32), page_limit[:, None, None]).astype(
        jnp.bfloat16
    )
    score_scale = 1.0 / head_dim**0.5
    head_eye = jnp.eye(heads_here, dtype=jnp.bfloat16)
    spread_queries = page_queries[:, :, :, None, :] * head_eye[None, None, :, :, None]
    scores = (
        jnp.einsum(
            "pkjhd,pthd->pkjt", spread_queries, cache_keys, preferred_element_type=jnp.float32
        )
        * score_scale
    )
    scores = jnp.where(in_range[:, None, None, :], scores, -jnp.inf)
    fresh_score = (
        jnp.einsum("pkhd,phd->pkh", page_queries, key_page, preferred_element_type=jnp.float32)
        * score_scale
    )
    page_top = jnp.max(scores, axis=3)
    owner_top = jnp.max(jnp.where(same_owner[:, :, None, None], page_top[None], -jnp.inf), axis=1)
    row_top = jnp.maximum(owner_top, fresh_score)
    weights = jnp.exp(scores - row_top[..., None])
    fresh_weight = jnp.exp(fresh_score - row_top)
    owned_float = owned_pages.astype(jnp.float32)
    denominator = jnp.einsum(
        "rp,pkh->rkh",
        owned_float,
        jnp.sum(weights, axis=3) + leader_float * fresh_weight,
        precision=lax.Precision.HIGHEST,
    )
    weights_rounded = weights.astype(jnp.bfloat16)
    fresh_rounded = lax.optimization_barrier(fresh_weight.astype(jnp.bfloat16)).astype(jnp.float32)
    page_context = jnp.einsum(
        "pkjt,pthd->pkjhd", weights_rounded, cache_values, preferred_element_type=jnp.float32
    )
    page_context = jnp.sum(page_context * head_eye.astype(jnp.float32)[None, None, :, :, None], axis=3)
    page_context = page_context + (leader_float * fresh_rounded)[..., None] * value_page.astype(
        jnp.float32
    )[:, None]
    accumulated = jnp.einsum(
        "rp,pkhd->rkhd", owned_float, page_context, precision=lax.Precision.HIGHEST
    )
    context = (accumulated / denominator[..., None]).astype(jnp.bfloat16)
    context_flat = context.reshape(row_count * choices_each, heads_here * head_dim)
    context_buf = jnp.dot(select_rows, context_flat, preferred_element_type=jnp.float32).astype(
        jnp.bfloat16
    )
    context_buf = context_buf.reshape(experts, capacity, heads_here, head_dim).transpose(0, 2, 1, 3)
    context_buf = context_buf.reshape(groups, pairs_here, capacity, head_dim)
    head_count = lax.axis_size("head")
    width_here = model_width // head_count
    wblocks = width_here // lanes
    partial_far = jnp.einsum(
        "spnh,phd->snd",
        lax.all_to_all(context_buf, "req", split_axis=0, concat_axis=0, tiled=True),
        output_weight,
        preferred_element_type=jnp.float32,
    )
    partial_far = partial_far.reshape(groups, capacity, head_count, wblocks, lanes).transpose(
        0, 2, 1, 3, 4
    )
    gate_flat = expert_gate.reshape(-1)
    spread = (
        jnp.where(select, gate_flat[None, :], jnp.float32(0.0))
        .reshape(experts * capacity, row_count, choices_each)
        .sum(axis=2)
        .T
    )
    alive_rows = live_mask.astype(jnp.float32)[:, None]
    returned = lax.all_to_all(
        partial_far.reshape(groups * head_count, capacity * wblocks, lanes),
        ("req", "head"),
        split_axis=0,
        concat_axis=0,
        tiled=True,
    )
    summed = returned.reshape(experts, replicas * head_count, capacity * wblocks, lanes).sum(axis=1)
    picked_rows = summed.reshape(experts * capacity, width_here)[target.reshape(row_count, choices_each)]
    result = jnp.sum(picked_rows * expert_gate[:, :, None], axis=1)
    return (result * alive_rows).astype(jnp.bfloat16)


def solution(mesh):
    return jax.shard_map(
        body,
        mesh=mesh,
        in_specs=(
            P("req", None),
            P(),
            P(None, "head", None, None),
            P("req", None, "head"),
            P("req", "head", None),
            P("req", None, "head", None),
            P("req", None, "head", None),
            P("req"),
            P("req", None),
            P("req", None),
            P("req", None),
            P("req"),
        ),
        out_specs=P("req", "head"),
        check_vma=False,
    )
```

```python
import jax
import jax.numpy as jnp
from jax import lax
from jax.sharding import PartitionSpec as P

AEXP = 8
CAP = 12


eps = 1e-06
theta = 10000.0


def rotate(vectors, positions):
    half_width = vectors.shape[-1] // 2
    frequency = theta ** (-(jnp.arange(half_width, dtype=jnp.float32) * 2.0) / vectors.shape[-1])
    angles = positions.astype(jnp.float32)[..., None] * frequency
    cosine = jnp.cos(angles)
    sine_part = jnp.sin(angles)
    first_half = vectors[..., :half_width]
    second = vectors[..., half_width:]
    return jnp.concatenate(
        [first_half * cosine - second * sine_part, second * cosine + first_half * sine_part],
        axis=-1,
    )


def body(
    tokens,
    norm_gain,
    key_value_weight,
    query_weight,
    output_weight,
    cache_keys,
    cache_values,
    cache_length,
    page_table,
    expert_choice,
    expert_gate,
    live_mask,
):
    groups = lax.axis_size("req")
    group_index = lax.axis_index("req")
    row_count = tokens.shape[0]
    model_width = tokens.shape[1]
    choices_each = expert_choice.shape[1]
    heads_here = key_value_weight.shape[1]
    head_dim = key_value_weight.shape[3]
    pairs_here = query_weight.shape[0]
    pages_here = cache_keys.shape[0]
    page_len = cache_keys.shape[1]
    max_pages = page_table.shape[1]
    experts = AEXP
    capacity = CAP
    as_float = tokens.astype(jnp.float32)
    normed = (
        as_float
        * lax.rsqrt(jnp.mean(as_float * as_float, axis=-1, keepdims=True) + eps)
        * norm_gain
    ).astype(jnp.bfloat16)
    choice_major = expert_choice.T.reshape(-1)
    onehot = (choice_major[:, None] == jnp.arange(experts)[None, :]).astype(jnp.int32)
    before = jnp.cumsum(onehot, axis=0) - onehot
    slot_index = jnp.sum(before * onehot, axis=1)
    target = (choice_major * capacity + slot_index).reshape(choices_each, row_count).T.reshape(-1)
    select = target[None, :] == jnp.arange(experts * capacity)[:, None]
    select_rows = select.astype(jnp.bfloat16)
    lanes = 128
    blocks = model_width // lanes
    repeated = jnp.repeat(normed, choices_each, axis=0).reshape(-1, blocks, lanes)
    sendbuf = jnp.einsum(
        "mr,rab->mab", select_rows, repeated, preferred_element_type=jnp.float32
    ).astype(jnp.bfloat16)
    replicas = groups // experts
    sendbuf = jnp.broadcast_to(
        sendbuf.reshape(experts, 1, capacity, blocks, lanes),
        (experts, replicas, capacity, blocks, lanes),
    )
    sendbuf = sendbuf.reshape(groups, capacity * blocks, lanes)
    tokens_far = lax.all_to_all(sendbuf, "req", split_axis=0, concat_axis=0, tiled=True)
    queries_far = jnp.einsum(
        "snab,pabh->spnh",
        tokens_far.reshape(groups, capacity, blocks, lanes),
        query_weight.reshape(pairs_here, blocks, lanes, head_dim),
        preferred_element_type=jnp.float32,
    ).astype(jnp.bfloat16)
    key_value = jnp.einsum(
        "rf,fhkd->rhkd", normed, key_value_weight, preferred_element_type=jnp.float32
    )
    key_new = rotate(key_value[:, :, 0], cache_length[:, None]).astype(jnp.bfloat16)
    value_new = key_value[:, :, 1].astype(jnp.bfloat16)
    local_ids = page_table - group_index * pages_here
    page_used = jnp.arange(max_pages)[None, :] * page_len < cache_length[:, None]
    page_match = page_used[:, :, None] & (
        local_ids[:, :, None] == jnp.arange(pages_here)[None, None, :]
    )
    owned_pages = jnp.any(page_match, axis=1)
    page_taken = jnp.any(owned_pages, axis=0)
    page_owner = jnp.sum(
        owned_pages.astype(jnp.int32) * jnp.arange(row_count, dtype=jnp.int32)[:, None], axis=0
    )
    page_start = jnp.sum(
        page_match.astype(jnp.int32)
        * (jnp.arange(max_pages, dtype=jnp.int32) * page_len)[None, :, None],
        axis=(0, 1),
    )
    page_limit = cache_length[page_owner]
    in_range = page_taken[:, None] & (
        page_start[:, None] + jnp.arange(page_len)[None, :] < page_limit[:, None]
    )
    queries = lax.all_to_all(queries_far, "req", split_axis=0, concat_axis=0, tiled=True)
    queries = (
        queries.reshape(experts, heads_here, capacity, head_dim)
        .transpose(0, 2, 1, 3)
        .reshape(experts * capacity, heads_here, head_dim)
    )
    page_slots = target.reshape(row_count, choices_each)[page_owner]
    key_page = key_new[page_owner]
    value_page = value_new[page_owner]
    same_owner = (
        page_taken[:, None] & page_taken[None, :] & (page_owner[:, None] == page_owner[None, :])
    )
    leader = jnp.any(local_ids[:, :1] == jnp.arange(pages_here)[None, :], axis=0)
    leader_float = leader.astype(jnp.float32)[:, None, None]
    page_raw = queries[page_slots]
    page_queries = rotate(page_raw.astype(jnp.float32), page_limit[:, None, None]).astype(
        jnp.bfloat16
    )
    score_scale = 1.0 / head_dim**0.5
    head_eye = jnp.eye(heads_here, dtype=jnp.bfloat16)
    spread_queries = page_queries[:, :, :, None, :] * head_eye[None, None, :, :, None]
    scores = (
        jnp.einsum(
            "pkjhd,pthd->pkjt", spread_queries, cache_keys, preferred_element_type=jnp.float32
        )
        * score_scale
    )
    scores = jnp.where(in_range[:, None, None, :], scores, -jnp.inf)
    fresh_score = (
        jnp.einsum("pkhd,phd->pkh", page_queries, key_page, preferred_element_type=jnp.float32)
        * score_scale
    )
    page_top = jnp.max(scores, axis=3)
    owner_top = jnp.max(jnp.where(same_owner[:, :, None, None], page_top[None], -jnp.inf), axis=1)
    row_top = jnp.maximum(owner_top, fresh_score)
    weights = jnp.exp(scores - row_top[..., None])
    fresh_weight = jnp.exp(fresh_score - row_top)
    owned_float = owned_pages.astype(jnp.float32)
    denominator = jnp.einsum(
        "rp,pkh->rkh",
        owned_float,
        jnp.sum(weights, axis=3) + leader_float * fresh_weight,
        precision=lax.Precision.HIGHEST,
    )
    weights_rounded = weights.astype(jnp.bfloat16)
    fresh_rounded = lax.optimization_barrier(fresh_weight.astype(jnp.bfloat16)).astype(jnp.float32)
    page_context = jnp.einsum(
        "pkjt,pthd->pkjhd", weights_rounded, cache_values, preferred_element_type=jnp.float32
    )
    page_context = jnp.sum(page_context * head_eye.astype(jnp.float32)[None, None, :, :, None], axis=3)
    page_context = page_context + (leader_float * fresh_rounded)[..., None] * value_page.astype(
        jnp.float32
    )[:, None]
    accumulated = jnp.einsum(
        "rp,pkhd->rkhd", owned_float, page_context, precision=lax.Precision.HIGHEST
    )
    context = (accumulated / denominator[..., None]).astype(jnp.bfloat16)
    context_flat = context.reshape(row_count * choices_each, heads_here * head_dim)
    context_buf = jnp.dot(select_rows, context_flat, preferred_element_type=jnp.float32).astype(
        jnp.bfloat16
    )
    context_buf = context_buf.reshape(experts, capacity, heads_here, head_dim).transpose(0, 2, 1, 3)
    context_buf = context_buf.reshape(groups, pairs_here, capacity, head_dim)
    head_count = lax.axis_size("head")
    width_here = model_width // head_count
    wblocks = width_here // lanes
    partial_far = jnp.einsum(
        "spnh,phd->snd",
        lax.all_to_all(context_buf, "req", split_axis=0, concat_axis=0, tiled=True),
        output_weight,
        preferred_element_type=jnp.float32,
    )
    partial_far = partial_far.reshape(groups, capacity, head_count, wblocks, lanes).transpose(
        0, 2, 1, 3, 4
    )
    gate_flat = expert_gate.reshape(-1)
    spread = (
        jnp.where(select, gate_flat[None, :], jnp.float32(0.0))
        .reshape(experts * capacity, row_count, choices_each)
        .sum(axis=2)
        .T
    )
    alive_rows = live_mask.astype(jnp.float32)[:, None]
    returned = lax.all_to_all(
        partial_far.reshape(groups * head_count, capacity * wblocks, lanes),
        ("req", "head"),
        split_axis=0,
        concat_axis=0,
        tiled=True,
    )
    summed = returned.reshape(experts, replicas * head_count, capacity * wblocks, lanes).sum(axis=1)
    result = jnp.einsum(
        "rm,mab->rab",
        spread,
        summed.reshape(experts * capacity, wblocks, lanes),
        precision=lax.Precision.HIGHEST,
    ).reshape(row_count, width_here)
    return (result * alive_rows).astype(jnp.bfloat16)


def solution(mesh):
    return jax.shard_map(
        body,
        mesh=mesh,
        in_specs=(
            P("req", None),
            P(),
            P(None, "head", None, None),
            P("req", None, "head"),
            P("req", "head", None),
            P("req", None, "head", None),
            P("req", None, "head", None),
            P("req"),
            P("req", None),
            P("req", None),
            P("req", None),
            P("req"),
        ),
        out_specs=P("req", "head"),
        check_vma=False,
    )
```

```python
import jax
import jax.numpy as jnp
from jax import lax
from jax.sharding import PartitionSpec as P

AEXP = 8
CAP = 12


eps = 1e-06
theta = 10000.0


def rotate(vectors, positions):
    half_width = vectors.shape[-1] // 2
    frequency = theta ** (-(jnp.arange(half_width, dtype=jnp.float32) * 2.0) / vectors.shape[-1])
    angles = positions.astype(jnp.float32)[..., None] * frequency
    cosine = jnp.cos(angles)
    sine_part = jnp.sin(angles)
    first_half = vectors[..., :half_width]
    second = vectors[..., half_width:]
    return jnp.concatenate(
        [first_half * cosine - second * sine_part, second * cosine + first_half * sine_part],
        axis=-1,
    )


def body(
    tokens,
    norm_gain,
    key_value_weight,
    query_weight,
    output_weight,
    cache_keys,
    cache_values,
    cache_length,
    page_table,
    expert_choice,
    expert_gate,
    live_mask,
):
    groups = lax.axis_size("req")
    group_index = lax.axis_index("req")
    row_count = tokens.shape[0]
    model_width = tokens.shape[1]
    choices_each = expert_choice.shape[1]
    heads_here = key_value_weight.shape[1]
    head_dim = key_value_weight.shape[3]
    pairs_here = query_weight.shape[0]
    pages_here = cache_keys.shape[0]
    page_len = cache_keys.shape[1]
    max_pages = page_table.shape[1]
    experts = AEXP
    capacity = CAP
    as_float = tokens.astype(jnp.float32)
    normed = (
        as_float
        * lax.rsqrt(jnp.mean(as_float * as_float, axis=-1, keepdims=True) + eps)
        * norm_gain
    ).astype(jnp.bfloat16)
    flat_expert = expert_choice.reshape(-1)
    onehot = (flat_expert[:, None] == jnp.arange(experts)[None, :]).astype(jnp.int32)
    before = jnp.cumsum(onehot, axis=0) - onehot
    slot_index = jnp.sum(before * onehot, axis=1)
    target = flat_expert * capacity + slot_index
    select = target[None, :] == jnp.arange(experts * capacity)[:, None]
    select_rows = select.astype(jnp.bfloat16)
    lanes = 128
    blocks = model_width // lanes
    repeated = jnp.repeat(normed, choices_each, axis=0).reshape(-1, blocks, lanes)
    sendbuf = jnp.einsum(
        "mr,rab->mab", select_rows, repeated, preferred_element_type=jnp.float32
    ).astype(jnp.bfloat16)
    replicas = groups // experts
    sendbuf = jnp.broadcast_to(
        sendbuf.reshape(experts, 1, capacity, blocks, lanes),
        (experts, replicas, capacity, blocks, lanes),
    )
    sendbuf = sendbuf.reshape(groups, capacity * blocks, lanes)
    tokens_far = lax.all_to_all(sendbuf, "req", split_axis=0, concat_axis=0, tiled=True)
    queries_far = jnp.einsum(
        "snab,pabh->spnh",
        tokens_far.reshape(groups, capacity, blocks, lanes),
        query_weight.reshape(pairs_here, blocks, lanes, head_dim),
        preferred_element_type=jnp.float32,
    ).astype(jnp.bfloat16)
    key_value = jnp.einsum(
        "rf,fhkd->rhkd", normed, key_value_weight, preferred_element_type=jnp.float32
    )
    key_new = rotate(key_value[:, :, 0], cache_length[:, None]).astype(jnp.bfloat16)
    value_new = key_value[:, :, 1].astype(jnp.bfloat16)
    local_ids = page_table - group_index * pages_here
    page_used = jnp.arange(max_pages)[None, :] * page_len < cache_length[:, None]
    page_match = page_used[:, :, None] & (
        local_ids[:, :, None] == jnp.arange(pages_here)[None, None, :]
    )
    owned_pages = jnp.any(page_match, axis=1)
    page_taken = jnp.any(owned_pages, axis=0)
    page_owner = jnp.sum(
        owned_pages.astype(jnp.int32) * jnp.arange(row_count, dtype=jnp.int32)[:, None], axis=0
    )
    page_start = jnp.sum(
        page_match.astype(jnp.int32)
        * (jnp.arange(max_pages, dtype=jnp.int32) * page_len)[None, :, None],
        axis=(0, 1),
    )
    page_limit = cache_length[page_owner]
    in_range = page_taken[:, None] & (
        page_start[:, None] + jnp.arange(page_len)[None, :] < page_limit[:, None]
    )
    queries = lax.all_to_all(queries_far, "req", split_axis=0, concat_axis=0, tiled=True)
    queries = (
        queries.reshape(experts, heads_here, capacity, head_dim)
        .transpose(0, 2, 1, 3)
        .reshape(experts * capacity, heads_here, head_dim)
    )
    page_slots = target.reshape(row_count, choices_each)[page_owner]
    key_page = key_new[page_owner]
    value_page = value_new[page_owner]
    same_owner = (
        page_taken[:, None] & page_taken[None, :] & (page_owner[:, None] == page_owner[None, :])
    )
    leader = jnp.any(local_ids[:, :1] == jnp.arange(pages_here)[None, :], axis=0)
    leader_float = leader.astype(jnp.float32)[:, None, None]
    page_raw = queries[page_slots]
    page_queries = rotate(page_raw.astype(jnp.float32), page_limit[:, None, None]).astype(
        jnp.bfloat16
    )
    score_scale = 1.0 / head_dim**0.5
    head_eye = jnp.eye(heads_here, dtype=jnp.bfloat16)
    spread_queries = page_queries[:, :, :, None, :] * head_eye[None, None, :, :, None]
    scores = (
        jnp.einsum(
            "pkjhd,pthd->pkjt", spread_queries, cache_keys, preferred_element_type=jnp.float32
        )
        * score_scale
    )
    scores = jnp.where(in_range[:, None, None, :], scores, -jnp.inf)
    fresh_score = (
        jnp.einsum("pkhd,phd->pkh", page_queries, key_page, preferred_element_type=jnp.float32)
        * score_scale
    )
    page_top = jnp.max(scores, axis=3)
    owner_top = jnp.max(jnp.where(same_owner[:, :, None, None], page_top[None], -jnp.inf), axis=1)
    row_top = jnp.maximum(owner_top, fresh_score)
    weights = jnp.exp(scores - row_top[..., None])
    fresh_weight = jnp.exp(fresh_score - row_top)
    owned_float = owned_pages.astype(jnp.float32)
    page_denominator = jnp.sum(weights, axis=3) + leader_float * fresh_weight
    weights_rounded = weights.astype(jnp.bfloat16)
    fresh_rounded = lax.optimization_barrier(fresh_weight.astype(jnp.bfloat16)).astype(jnp.float32)
    page_context = jnp.einsum(
        "pkjt,pthd->pkjhd", weights_rounded, cache_values, preferred_element_type=jnp.float32
    )
    page_context = jnp.sum(page_context * head_eye.astype(jnp.float32)[None, None, :, :, None], axis=3)
    page_context = page_context + (leader_float * fresh_rounded)[..., None] * value_page.astype(
        jnp.float32
    )[:, None]
    both = jnp.einsum(
        "rp,pkhd->rkhd",
        owned_float,
        jnp.concatenate([page_context, page_denominator[..., None]], axis=3),
        precision=lax.Precision.HIGHEST,
    )
    accumulated = both[..., :head_dim]
    denominator = both[..., head_dim]
    context = (accumulated / denominator[..., None]).astype(jnp.bfloat16)
    context_flat = context.reshape(row_count * choices_each, heads_here * head_dim)
    context_buf = jnp.dot(select_rows, context_flat, preferred_element_type=jnp.float32).astype(
        jnp.bfloat16
    )
    context_buf = context_buf.reshape(experts, capacity, heads_here, head_dim).transpose(0, 2, 1, 3)
    context_buf = context_buf.reshape(groups, pairs_here, capacity, head_dim)
    head_count = lax.axis_size("head")
    width_here = model_width // head_count
    wblocks = width_here // lanes
    partial_far = jnp.einsum(
        "spnh,phd->snd",
        lax.all_to_all(context_buf, "req", split_axis=0, concat_axis=0, tiled=True),
        output_weight,
        preferred_element_type=jnp.float32,
    )
    partial_far = partial_far.reshape(groups, capacity, head_count, wblocks, lanes).transpose(
        0, 2, 1, 3, 4
    )
    gate_flat = expert_gate.reshape(-1)
    spread = (
        jnp.where(select, gate_flat[None, :], jnp.float32(0.0))
        .reshape(experts * capacity, row_count, choices_each)
        .sum(axis=2)
        .T
    )
    alive_rows = live_mask.astype(jnp.float32)[:, None]
    returned = lax.all_to_all(
        partial_far.reshape(groups * head_count, capacity * wblocks, lanes),
        ("req", "head"),
        split_axis=0,
        concat_axis=0,
        tiled=True,
    )
    summed = returned.reshape(experts, replicas * head_count, capacity * wblocks, lanes).sum(axis=1)
    result = jnp.einsum(
        "rm,mab->rab",
        spread,
        summed.reshape(experts * capacity, wblocks, lanes),
        precision=lax.Precision.HIGHEST,
    ).reshape(row_count, width_here)
    return (result * alive_rows).astype(jnp.bfloat16)


def solution(mesh):
    return jax.shard_map(
        body,
        mesh=mesh,
        in_specs=(
            P("req", None),
            P(),
            P(None, "head", None, None),
            P("req", None, "head"),
            P("req", "head", None),
            P("req", None, "head", None),
            P("req", None, "head", None),
            P("req"),
            P("req", None),
            P("req", None),
            P("req", None),
            P("req"),
        ),
        out_specs=P("req", "head"),
        check_vma=False,
    )
```
